128 devices in a mesh: seq: 16 (over y_hi, z, core), mp: 8 (over y_lo, x).
Axes of the slice: x: 4, y: 4 (y_hi: 2, y_lo: 2; y = y_hi * 2 + y_lo), z: 4, core: 2. Of those that a mesh axis runs over, the one named last changes fastest.
Arguments:
- tokens_in: bfloat16 [32768, 2048], P('seq'), may hold values from -6 to 6
- norm_gain: float32 [2048], replicated, may hold values from 0.5 to 200
- q_weight: bfloat16 [2048, 2048], P('seq', 'mp'), may hold values from -0.125 to 0.125
- kv_weight: bfloat16 [4, 2048, 128], P(None, 'seq'), may hold values from -0.125 to 0.125
- out_weight: bfloat16 [2048, 2048], P('seq', 'mp'), may hold values from -0.25 to 0.25
- segment_ids: int32 [32768], P('seq'), may hold values from 0 to 31, never falling along the last dimension, each value on 1 to 8192 neighbouring positions
- page_table: int32 [256], P('seq'), may hold values from 0 to 255, as said below
Outputs:
- layer_out: bfloat16 [32768, 2048], P('seq', 'mp')
- kv_cache: bfloat16 [256, 512, 128], P('seq', 'mp')
The draws below stay inside these ranges and needn't reach their ends.
Inputs may be any that keep to these rules, and one draw needn't show every extreme that they name: `segment_ids`: segment numbers never fall along the stream; each of the 32 segments holds 1 to 8192 tokens and one holds exactly 8192. `page_table`: A permutation of the 256 cache slots; slot s belongs to index s // 16 of seq. The pages of index i of seq go to the indices i + o, counted round, for 16 distinct offsets o that are the same for every i, among them 1 and 16 / 2; exactly 1 pages to each owner.
All inputs are finite; a program needn't handle non-finite values.
Results may differ from the reference program's by a relative error of at most 0.018.
The reference program's roundings to bfloat16 on the way count: a program that leaves them out, or rounds other values in their place, can miss the bound.
Values may be sent and summed in bfloat16 or wider, within the bound.
No kernel may reach another device: no remote copies, remote signals or barrier semaphores. Data moves between devices by JAX's collectives and lax.ppermute only.
A program may use at most 64 MiB of HBM per device.

```python
import math
import jax
import jax.numpy as jnp
import numpy as np
from jax import lax

D = 2048
H = 32
HD = 64
KVH = 4
W = 2048
PAGE = 128
TOK_DEV = 2048
TOKENS = 32768
SEGS = 32
MOST = 8192
PAGES_DEV = 16
NPAGES = 256
SPREAD = 16
CAP = 1
N_SEQ = 16
N_MP = 8


def draw_norm_gain(key, part):
    first_key = jax.random.fold_in(key, 0)
    gains = jnp.exp(jax.random.uniform(first_key, (D,), jnp.float32, math.log(0.5), math.log(2.0)))
    return gains


def draw_page_table(key, part):
    first_key, second_key = jax.random.split(key)
    order_all = jax.random.permutation(first_key, N_SEQ).astype(jnp.int32)
    where_one = jnp.argmax(order_all == 1)
    order_all = order_all.at[where_one].set(order_all[0])
    order_all = order_all.at[0].set(1)
    halfway = N_SEQ // 2
    if halfway != 1:
        where_half = jnp.argmax(order_all == halfway)
        order_all = order_all.at[where_half].set(order_all[1])
        order_all = order_all.at[1].set(halfway)
    offsets = order_all[:SPREAD]
    lane_keys = jax.random.split(second_key, N_SEQ)
    lanes = jax.vmap(lambda one_key: jax.random.permutation(one_key, PAGES_DEV))(lane_keys).astype(jnp.int32)
    sources = jnp.arange(N_SEQ, dtype=jnp.int32)[:, None]
    hops = lanes // CAP
    owners = (sources + offsets[hops]) % N_SEQ
    slots = owners * PAGES_DEV + hops * CAP + lanes % CAP
    return slots.reshape(-1).astype(jnp.int32)


def level_of(own_key, shape, shards, smallest, top_value):
    level, own = 1.0, jax.random.fold_in(own_key, 6)
    for position, parts in shards:
        steps = jnp.exp(jax.random.uniform(jax.random.fold_in(own, position), (parts,), jnp.float32, smallest / len(shards), top_value / len(shards)))
        level = level * jnp.repeat(steps, shape[position] // parts).reshape([-1 if axis == position else 1 for axis in range(len(shape))])
    return level


def profile(number_of, total, limit, lean):
    weights = [(1 << 20) // math.isqrt(rank ** lean) + 1 for rank in range(2, number_of + 1)]
    spare, counts = total - limit - (number_of - 1), [1] * (number_of - 1)
    while spare > 0:
        movable = [i for i in range(number_of - 1) if counts[i] < limit]
        whole, remaining = sum([weights[i] for i in movable]), spare
        for i in movable:
            more = min(limit - counts[i], max(1, remaining * weights[i] // whole), spare)
            counts[i] = counts[i] + more
            spare = spare - more
    return np.array([limit] + counts)


def uneven(stream_key, number_of, total, bound, slope):
    if number_of == 2:
        one = jax.random.randint(stream_key, (), max(1, total - bound), min(bound, total - 1) + 1)
        return jnp.stack([one, total - one])
    sizes = jnp.asarray(profile(number_of, total, bound, slope), jnp.int32)
    couples = (number_of - 1) // 2
    giver, sink = sizes[1:1 + 2 * couples:2], sizes[2:2 + 2 * couples:2]
    slack = jnp.minimum(giver - 1, bound - sink)
    shifted = jax.random.randint(jax.random.fold_in(stream_key, 1), (couples,), 0, 1 << 20) % (slack + 1)
    sizes = sizes.at[1:1 + 2 * couples:2].set(giver - shifted).at[2:2 + 2 * couples:2].set(sink + shifted)
    return sizes[jax.random.permutation(jax.random.fold_in(stream_key, 2), number_of)]


def normal_values(key, extent, deviation, limit, pieces=(), held_as=jnp.bfloat16):
    level = level_of(key, extent, pieces, -0.22, 0.18) if pieces else 1.0
    entries = jax.random.normal(key, extent, jnp.float32) * deviation * level
    return jnp.minimum(jnp.maximum(entries, -limit), limit).astype(held_as)


def setup_inputs(seed: int = 0) -> dict:
    streams_of = jax.random.split(jax.random.key(seed), 8)
    tokens_in = normal_values(streams_of[0], (TOKENS, D), 1.0, 6.0, ((0, 16),))
    norm_gain = draw_norm_gain(jax.random.fold_in(streams_of[7], 71), 0)
    q_weight = normal_values(streams_of[2], (D, H * HD), D ** -0.5, 0.125, ((0, 16), (1, 8)))
    kv_weight = normal_values(streams_of[3], (KVH, D, 2 * HD), D ** -0.5, 0.125, ((1, 16),))
    out_weight = normal_values(streams_of[4], (D, H * HD), (H * HD // 4) ** -0.5, 0.25, ((0, 16), (1, 8)))
    segment_ids = jnp.searchsorted(jnp.cumsum(uneven(streams_of[5], SEGS, TOKENS, MOST, 2)), jnp.arange(TOKENS), side="right").astype(jnp.int32)
    page_table = draw_page_table(jax.random.fold_in(streams_of[7], 71), 0)
    return {"tokens_in": tokens_in, "norm_gain": norm_gain, "q_weight": q_weight, "kv_weight": kv_weight, "out_weight": out_weight, "segment_ids": segment_ids, "page_table": page_table}


def rotate_half(values, cosine, sine_table):
    half = values.shape[-1] // 2
    first_half = values[..., :half]
    second = values[..., half:]
    return jnp.concatenate([first_half * cosine - second * sine_table, second * cosine + first_half * sine_table], axis=-1)

def angle_tables(positions):
    half = HD // 2
    freqs = jnp.exp(jnp.arange(half, dtype=jnp.float32) * (-2.0 * math.log(10000.0) / HD))
    angles = positions.astype(jnp.float32)[:, None] * freqs[None, :]
    return (jnp.cos(angles), jnp.sin(angles))

def reference(tokens_in, norm_gain, q_weight, kv_weight, out_weight, segment_ids, page_table):
    inputs = tokens_in.astype(jnp.float32)
    meansq = lax.optimization_barrier(jnp.mean(inputs * inputs, axis=-1, keepdims=True))
    normed = (inputs * lax.rsqrt(meansq + 1e-05) * norm_gain).astype(jnp.bfloat16)
    indices = jnp.arange(TOKENS, dtype=jnp.int32)
    boundary = jnp.concatenate([jnp.ones((1,), bool), segment_ids[1:] != segment_ids[:-1]])
    starts = lax.cummax(jnp.where(boundary, indices, jnp.int32(0)), axis=0)
    positions = indices - starts
    cosine, sine_table = angle_tables(positions)
    queries = jnp.dot(normed, q_weight, preferred_element_type=jnp.float32).reshape(TOKENS, H, HD)
    queries = rotate_half(queries, cosine[:, None, :], sine_table[:, None, :]).astype(jnp.bfloat16)
    kv_flat = kv_weight.transpose(1, 0, 2).reshape(D, KVH * 2 * HD)
    projected = jnp.dot(normed, kv_flat, preferred_element_type=jnp.float32).reshape(TOKENS, KVH, 2 * HD)
    key_rows = rotate_half(projected[..., :HD], cosine[:, None, :], sine_table[:, None, :]).astype(jnp.bfloat16)
    value_rows = projected[..., HD:].astype(jnp.bfloat16)
    group = H // KVH
    block_rows = min(512, TOK_DEV)
    blocks = TOKENS // block_rows
    key_padded = jnp.concatenate([jnp.zeros((W, KVH, HD), jnp.bfloat16), key_rows], axis=0)
    value_padded = jnp.concatenate([jnp.zeros((W, KVH, HD), jnp.bfloat16), value_rows], axis=0)
    scale = 1.0 / math.sqrt(HD)

    def one_block(block):
        row_first = block * block_rows
        query_block = lax.dynamic_slice_in_dim(queries, row_first, block_rows, 0).astype(jnp.float32)
        query_block = query_block.reshape(block_rows, KVH, group, HD)
        key_block = lax.dynamic_slice_in_dim(key_padded, row_first, W + block_rows, 0).astype(jnp.float32)
        value_block = lax.dynamic_slice_in_dim(value_padded, row_first, W + block_rows, 0).astype(jnp.float32)
        key_index = row_first - W + jnp.arange(W + block_rows, dtype=jnp.int32)
        query_index = row_first + jnp.arange(block_rows, dtype=jnp.int32)
        query_start = lax.dynamic_slice_in_dim(starts, row_first, block_rows, 0)
        scores = jnp.einsum('qjgd,kjd->jgqk', query_block, key_block) * scale
        keep = (key_index[None, :] >= query_start[:, None]) & (key_index[None, :] <= query_index[:, None])
        keep = keep & (query_index[:, None] - key_index[None, :] < W)
        masked = jnp.where(keep[None, None], scores, -1e+30)
        highest = lax.optimization_barrier(jnp.max(masked, axis=-1, keepdims=True))
        weights = jnp.where(keep[None, None], jnp.exp(masked - highest), 0.0)
        probs = (weights / lax.optimization_barrier(jnp.sum(weights, axis=-1, keepdims=True))).astype(jnp.bfloat16)
        mixed = jnp.einsum('jgqk,kjd->qjgd', probs.astype(jnp.float32), value_block)
        return mixed.reshape(block_rows, H * HD).astype(jnp.bfloat16)
    attended = lax.map(one_block, jnp.arange(blocks, dtype=jnp.int32)).reshape(TOKENS, H * HD)
    columns = H * HD // N_MP
    total = jnp.zeros((TOKENS, D), jnp.float32)
    for group_index in range(N_MP):
        lower = group_index * columns
        partial_term = jnp.dot(attended[:, lower:lower + columns], out_weight[:, lower:lower + columns].T, preferred_element_type=jnp.float32)
        rounded = lax.optimization_barrier(partial_term.astype(jnp.bfloat16))
        total = total + rounded.astype(jnp.float32)
    layer_out = total.astype(jnp.bfloat16)
    combined = jnp.concatenate([key_rows, value_rows], axis=-1).reshape(TOKENS, KVH * 2 * HD)
    page_blocks = combined.reshape(NPAGES, PAGE, KVH * 2 * HD).transpose(0, 2, 1)
    kv_cache = jnp.zeros_like(page_blocks).at[page_table].set(page_blocks)
    return (layer_out, kv_cache)
```

```python
import math

import jax
import jax.numpy as jnp
from jax import lax
from jax.sharding import PartitionSpec as P

W = 2048
PAGE = 128
SEGS = 32


def from_behind(x, axis, by):
    peers = lax.axis_size(axis)
    pairs = [(i, i + by) for i in range(peers) if 0 <= i + by < peers]
    return lax.ppermute(x, axis, pairs)


def shift_round(x, axis, by):
    peers = lax.axis_size(axis)
    return lax.ppermute(x, axis, [(i, (i + by) % peers) for i in range(peers)])


def rotate_half(values, cosine, sine_table):
    half = values.shape[-1] // 2
    first_half = values[..., :half]
    second = values[..., half:]
    return jnp.concatenate(
        [first_half * cosine - second * sine_table, second * cosine + first_half * sine_table],
        axis=-1,
    )


def attend_piece(carry, piece, start, queries, query_first, query_start, block_rows):
    head_size = queries.shape[2]
    count = piece.shape[0]
    key_rows = piece[:, :head_size]
    value_rows = piece[:, head_size:]
    key_index = start + jnp.arange(count, dtype=jnp.int32)
    scale = 1.0 / math.sqrt(head_size)
    blocks = queries.shape[0] // block_rows

    def one_block(block, state):
        row_first = block * block_rows
        query_block = lax.dynamic_slice_in_dim(queries, row_first, block_rows, 0)
        query_index = query_first + row_first + jnp.arange(block_rows, dtype=jnp.int32)
        query_begin = lax.dynamic_slice_in_dim(query_start, row_first, block_rows, 0)
        lowest = jnp.maximum(query_begin[0], query_index[0] - W + 1)
        live = (start <= query_index[-1]) & (start + count - 1 >= lowest)

        def compute(inner):
            best, totals, accum = inner
            best_block = lax.dynamic_slice_in_dim(best, row_first, block_rows, 1)
            total_block = lax.dynamic_slice_in_dim(totals, row_first, block_rows, 1)
            accum_block = lax.dynamic_slice_in_dim(accum, row_first, block_rows, 1)
            scores = (
                jnp.einsum("qhd,kd->hqk", query_block, key_rows, preferred_element_type=jnp.float32)
                * scale
            )
            keep = (key_index[None, :] >= query_begin[:, None]) & (
                key_index[None, :] <= query_index[:, None]
            )
            keep = keep & (query_index[:, None] - key_index[None, :] < W)
            masked = jnp.where(keep[None], scores, -1e30)
            new_best = jnp.maximum(best_block, jnp.max(masked, axis=-1))
            weights = jnp.where(keep[None], jnp.exp(masked - new_best[..., None]), 0.0)
            factor = jnp.exp(best_block - new_best)
            new_total = total_block * factor + jnp.sum(weights, axis=-1)
            mixed = jnp.einsum(
                "hqk,kd->hqd",
                weights.astype(jnp.bfloat16),
                value_rows,
                preferred_element_type=jnp.float32,
            )
            new_accum = accum_block * factor[..., None] + mixed
            best = lax.dynamic_update_slice_in_dim(best, new_best, row_first, 1)
            totals = lax.dynamic_update_slice_in_dim(totals, new_total, row_first, 1)
            accum = lax.dynamic_update_slice_in_dim(accum, new_accum, row_first, 1)
            return (best, totals, accum)

        return lax.cond(live, compute, lambda inner: inner, state)

    return lax.fori_loop(0, blocks, one_block, carry)


def body(tokens_in, norm_gain, q_weight, kv_weight, out_weight, segment_ids, page_table):
    seq_count = lax.axis_size("seq")
    mp_count = lax.axis_size("mp")
    seq_index = lax.axis_index("seq")
    mp_index = lax.axis_index("mp")
    tok_rows = tokens_in.shape[0]
    kv_heads = kv_weight.shape[0]
    head_size = kv_weight.shape[2] // 2
    ratio = mp_count // kv_heads
    own_head = mp_index // ratio
    kv_own = lax.dynamic_index_in_dim(kv_weight, own_head, 0, keepdims=False)
    q_columns = q_weight.shape[1]
    w_inputs = lax.all_gather(
        jnp.concatenate([q_weight, kv_own], axis=1), "seq", axis=0, tiled=True
    )
    w_output = lax.all_gather(out_weight, "seq", axis=0, tiled=True)
    inputs = tokens_in.astype(jnp.float32)
    meansq = jnp.mean(inputs * inputs, axis=-1, keepdims=True)
    normed = (inputs * lax.rsqrt(meansq + 1e-05) * norm_gain).astype(jnp.bfloat16)
    token_first = seq_index * tok_rows
    global_index = token_first + jnp.arange(tok_rows, dtype=jnp.int32)
    seg_values = jnp.arange(SEGS, dtype=jnp.int32)
    seg_hist = jnp.sum((segment_ids[:, None] == seg_values[None, :]).astype(jnp.int32), axis=0)
    seg_total = lax.psum(seg_hist, "seq")
    seg_first = jnp.cumsum(seg_total) - seg_total
    query_start = jnp.sum(
        jnp.where(segment_ids[:, None] == seg_values[None, :], seg_first[None, :], 0), axis=1
    )
    positions = global_index - query_start
    half = head_size // 2
    freqs = jnp.exp(jnp.arange(half, dtype=jnp.float32) * (-2.0 * math.log(10000.0) / head_size))
    angles = positions.astype(jnp.float32)[:, None] * freqs[None, :]
    cosine = jnp.cos(angles)
    sine_table = jnp.sin(angles)
    local_heads = q_columns // head_size
    projected_all = jnp.dot(normed, w_inputs, preferred_element_type=jnp.float32)
    queries = projected_all[:, :q_columns].reshape(tok_rows, local_heads, head_size)
    queries = rotate_half(queries, cosine[:, None, :], sine_table[:, None, :]).astype(jnp.bfloat16)
    projected = projected_all[:, q_columns:]
    key_rows = rotate_half(projected[:, :head_size], cosine, sine_table).astype(jnp.bfloat16)
    value_rows = projected[:, head_size:].astype(jnp.bfloat16)
    keyval = jnp.concatenate([key_rows, value_rows], axis=1)
    block_rows = min(512, tok_rows)
    initial = (
        jnp.full((local_heads, tok_rows), -1e30, jnp.float32),
        jnp.zeros((local_heads, tok_rows), jnp.float32),
        jnp.zeros((local_heads, tok_rows, head_size), jnp.float32),
    )

    def fold_piece(carry, piece, start):
        return attend_piece(carry, piece, start, queries, token_first, query_start, block_rows)

    state = fold_piece(initial, keyval, token_first)
    earlier = from_behind(keyval, "seq", 1)
    state = fold_piece(state, earlier, token_first - tok_rows)
    best, totals, accum = state
    attended = (
        (accum / totals[..., None])
        .transpose(1, 0, 2)
        .reshape(tok_rows, local_heads * head_size)
        .astype(jnp.bfloat16)
    )
    partial_term = lax.dot_general(
        attended, w_output, (((1,), (1,)), ((), ())), preferred_element_type=jnp.float32
    )
    layer_out = lax.psum_scatter(
        partial_term.astype(jnp.bfloat16), "mp", scatter_dimension=1, tiled=True
    )
    pages_dev = tok_rows // PAGE
    share_width = 2 * head_size // ratio
    share_index = mp_index % ratio
    share = lax.dynamic_slice_in_dim(keyval, share_index * share_width, share_width, 1)
    page_blocks = share.reshape(pages_dev, PAGE, share_width).transpose(0, 2, 1)
    owners = page_table // pages_dev
    local_slot = page_table % pages_dev
    spread = min(seq_count, pages_dev)
    capacity = pages_dev // spread
    page_order = jnp.arange(pages_dev, dtype=jnp.int32)
    same_owner = (owners[:, None] == owners[None, :]) & (page_order[None, :] < page_order[:, None])
    ranking = jnp.sum(same_owner.astype(jnp.int32), axis=1)
    lanes_all = seq_count * capacity
    send_lane = ((owners - seq_index) % seq_count) * capacity + ranking
    select = jnp.arange(lanes_all, dtype=jnp.int32)[:, None] == send_lane[None, :]
    outgoing = jnp.einsum(
        "sp,pfk->sfk", select.astype(jnp.bfloat16), page_blocks, preferred_element_type=jnp.float32
    ).astype(jnp.bfloat16)
    labels = jnp.sum(jnp.where(select, (local_slot + 1)[None, :], 0), axis=1)
    label_rows = jnp.broadcast_to(labels.astype(jnp.bfloat16)[:, None, None], (lanes_all, 1, PAGE))
    payload = jnp.concatenate([outgoing, label_rows], axis=1)
    arrived = [payload[:capacity]]
    for offset in range(1, seq_count):
        lanes = slice(offset * capacity, (offset + 1) * capacity)
        arrived.append(shift_round(payload[lanes], "seq", offset))
    landed = jnp.concatenate(arrived, axis=0)
    incoming = landed[:, :share_width]
    tags = landed[:, share_width, 0].astype(jnp.int32)
    placement = (tags[None, :] == (page_order + 1)[:, None]).astype(jnp.bfloat16)
    kv_cache = jnp.einsum(
        "ps,sfk->pfk", placement, incoming, preferred_element_type=jnp.float32
    ).astype(jnp.bfloat16)
    return (layer_out, kv_cache)


def solution(mesh):
    placed = (
        P("seq", None),
        P(),
        P("seq", "mp"),
        P(None, "seq", None),
        P("seq", "mp"),
        P("seq"),
        P("seq"),
    )
    return jax.shard_map(
        body,
        mesh=mesh,
        in_specs=placed,
        out_specs=(P("seq", "mp"), P("seq", "mp", None)),
        check_vma=False,
    )
```

```python
import math

import jax
import jax.numpy as jnp
from jax import lax
from jax.sharding import PartitionSpec as P

W = 2048
PAGE = 128
SEGS = 32


def from_behind(x, axis, by):
    peers = lax.axis_size(axis)
    pairs = [(i, i + by) for i in range(peers) if 0 <= i + by < peers]
    return lax.ppermute(x, axis, pairs)


def shift_round(x, axis, by):
    peers = lax.axis_size(axis)
    return lax.ppermute(x, axis, [(i, (i + by) % peers) for i in range(peers)])


def rotate_half(values, cosine, sine_table):
    half = values.shape[-1] // 2
    first_half = values[..., :half]
    second = values[..., half:]
    return jnp.concatenate(
        [first_half * cosine - second * sine_table, second * cosine + first_half * sine_table],
        axis=-1,
    )


def attend_piece(carry, piece, start, queries, query_first, query_start, block_rows):
    head_size = queries.shape[2]
    count = piece.shape[0]
    key_rows = piece[:, :head_size]
    value_rows = piece[:, head_size:]
    key_index = start + jnp.arange(count, dtype=jnp.int32)
    scale = 1.0 / math.sqrt(head_size)
    blocks = queries.shape[0] // block_rows

    def one_block(block, state):
        row_first = block * block_rows
        query_block = lax.dynamic_slice_in_dim(queries, row_first, block_rows, 0)
        query_index = query_first + row_first + jnp.arange(block_rows, dtype=jnp.int32)
        query_begin = lax.dynamic_slice_in_dim(query_start, row_first, block_rows, 0)
        lowest = jnp.maximum(query_begin[0], query_index[0] - W + 1)
        live = (start <= query_index[-1]) & (start + count - 1 >= lowest)

        def compute(inner):
            best, totals, accum = inner
            best_block = lax.dynamic_slice_in_dim(best, row_first, block_rows, 1)
            total_block = lax.dynamic_slice_in_dim(totals, row_first, block_rows, 1)
            accum_block = lax.dynamic_slice_in_dim(accum, row_first, block_rows, 1)
            scores = (
                jnp.einsum("qhd,kd->hqk", query_block, key_rows, preferred_element_type=jnp.float32)
                * scale
            )
            keep = (key_index[None, :] >= query_begin[:, None]) & (
                key_index[None, :] <= query_index[:, None]
            )
            keep = keep & (query_index[:, None] - key_index[None, :] < W)
            masked = jnp.where(keep[None], scores, -1e30)
            new_best = jnp.maximum(best_block, jnp.max(masked, axis=-1))
            weights = jnp.where(keep[None], jnp.exp(masked - new_best[..., None]), 0.0)
            factor = jnp.exp(best_block - new_best)
            new_total = total_block * factor + jnp.sum(weights, axis=-1)
            mixed = jnp.einsum(
                "hqk,kd->hqd",
                weights.astype(jnp.bfloat16),
                value_rows,
                preferred_element_type=jnp.float32,
            )
            new_accum = accum_block * factor[..., None] + mixed
            best = lax.dynamic_update_slice_in_dim(best, new_best, row_first, 1)
            totals = lax.dynamic_update_slice_in_dim(totals, new_total, row_first, 1)
            accum = lax.dynamic_update_slice_in_dim(accum, new_accum, row_first, 1)
            return (best, totals, accum)

        return lax.cond(live, compute, lambda inner: inner, state)

    return lax.fori_loop(0, blocks, one_block, carry)


def body(tokens_in, norm_gain, q_weight, kv_weight, out_weight, segment_ids, page_table):
    seq_count = lax.axis_size("seq")
    mp_count = lax.axis_size("mp")
    seq_index = lax.axis_index("seq")
    mp_index = lax.axis_index("mp")
    tok_rows = tokens_in.shape[0]
    kv_heads = kv_weight.shape[0]
    head_size = kv_weight.shape[2] // 2
    ratio = mp_count // kv_heads
    own_head = mp_index // ratio
    kv_own = lax.dynamic_index_in_dim(kv_weight, own_head, 0, keepdims=False)
    q_columns = q_weight.shape[1]
    w_inputs = lax.all_gather(
        jnp.concatenate([q_weight, kv_own], axis=1), "seq", axis=0, tiled=True
    )
    w_output = lax.all_gather(out_weight, "seq", axis=0, tiled=True)
    inputs = tokens_in.astype(jnp.float32)
    meansq = jnp.mean(inputs * inputs, axis=-1, keepdims=True)
    normed = (inputs * lax.rsqrt(meansq + 1e-05) * norm_gain).astype(jnp.bfloat16)
    token_first = seq_index * tok_rows
    global_index = token_first + jnp.arange(tok_rows, dtype=jnp.int32)
    seg_values = jnp.arange(SEGS, dtype=jnp.int32)
    seg_hist = jnp.sum((segment_ids[:, None] == seg_values[None, :]).astype(jnp.int32), axis=0)
    seg_total = lax.psum(seg_hist, "seq")
    seg_first = jnp.cumsum(seg_total) - seg_total
    query_start = jnp.sum(
        jnp.where(segment_ids[:, None] == seg_values[None, :], seg_first[None, :], 0), axis=1
    )
    positions = global_index - query_start
    half = head_size // 2
    freqs = jnp.exp(jnp.arange(half, dtype=jnp.float32) * (-2.0 * math.log(10000.0) / head_size))
    angles = positions.astype(jnp.float32)[:, None] * freqs[None, :]
    cosine = jnp.cos(angles)
    sine_table = jnp.sin(angles)
    local_heads = q_columns // head_size
    projected_all = jnp.dot(normed, w_inputs, preferred_element_type=jnp.float32)
    queries = projected_all[:, :q_columns].reshape(tok_rows, local_heads, head_size)
    queries = rotate_half(queries, cosine[:, None, :], sine_table[:, None, :]).astype(jnp.bfloat16)
    projected = projected_all[:, q_columns:]
    key_rows = rotate_half(projected[:, :head_size], cosine, sine_table).astype(jnp.bfloat16)
    value_rows = projected[:, head_size:].astype(jnp.bfloat16)
    keyval = jnp.concatenate([key_rows, value_rows], axis=1)
    block_rows = min(512, tok_rows)
    initial = (
        jnp.full((local_heads, tok_rows), -1e30, jnp.float32),
        jnp.zeros((local_heads, tok_rows), jnp.float32),
        jnp.zeros((local_heads, tok_rows, head_size), jnp.float32),
    )

    def fold_piece(carry, piece, start):
        return attend_piece(carry, piece, start, queries, token_first, query_start, block_rows)

    state = fold_piece(initial, keyval, token_first)
    earlier = from_behind(keyval, "seq", 1)
    state = fold_piece(state, earlier, token_first - tok_rows)
    best, totals, accum = state
    attended = (
        (accum / totals[..., None])
        .transpose(1, 0, 2)
        .reshape(tok_rows, local_heads * head_size)
        .astype(jnp.bfloat16)
    )
    partial_term = lax.dot_general(
        attended, w_output, (((1,), (1,)), ((), ())), preferred_element_type=jnp.float32
    )
    out_width = partial_term.shape[1] // mp_count
    partial_groups = partial_term.astype(jnp.bfloat16).reshape(tok_rows, mp_count, out_width)
    summed = partial_groups[:, mp_index].astype(jnp.float32)
    for offset in range(1, mp_count):
        target = (mp_index + offset) % mp_count
        sent = shift_round(partial_groups[:, target], "mp", offset)
        summed = summed + sent.astype(jnp.float32)
    layer_out = summed.astype(jnp.bfloat16)
    pages_dev = tok_rows // PAGE
    share_width = 2 * head_size // ratio
    share_index = mp_index % ratio
    share = lax.dynamic_slice_in_dim(keyval, share_index * share_width, share_width, 1)
    page_blocks = share.reshape(pages_dev, PAGE, share_width).transpose(0, 2, 1)
    owners = page_table // pages_dev
    local_slot = page_table % pages_dev
    spread = min(seq_count, pages_dev)
    capacity = pages_dev // spread
    page_order = jnp.arange(pages_dev, dtype=jnp.int32)
    same_owner = (owners[:, None] == owners[None, :]) & (page_order[None, :] < page_order[:, None])
    ranking = jnp.sum(same_owner.astype(jnp.int32), axis=1)
    lanes_all = seq_count * capacity
    send_lane = ((owners - seq_index) % seq_count) * capacity + ranking
    select = jnp.arange(lanes_all, dtype=jnp.int32)[:, None] == send_lane[None, :]
    outgoing = jnp.einsum(
        "sp,pfk->sfk", select.astype(jnp.bfloat16), page_blocks, preferred_element_type=jnp.float32
    ).astype(jnp.bfloat16)
    labels = jnp.sum(jnp.where(select, (local_slot + 1)[None, :], 0), axis=1)
    label_rows = jnp.broadcast_to(labels.astype(jnp.bfloat16)[:, None, None], (lanes_all, 1, PAGE))
    payload = jnp.concatenate([outgoing, label_rows], axis=1)
    arrived = [payload[:capacity]]
    for offset in range(1, seq_count):
        lanes = slice(offset * capacity, (offset + 1) * capacity)
        arrived.append(shift_round(payload[lanes], "seq", offset))
    landed = jnp.concatenate(arrived, axis=0)
    incoming = landed[:, :share_width]
    tags = landed[:, share_width, 0].astype(jnp.int32)
    placement = (tags[None, :] == (page_order + 1)[:, None]).astype(jnp.bfloat16)
    kv_cache = jnp.einsum(
        "ps,sfk->pfk", placement, incoming, preferred_element_type=jnp.float32
    ).astype(jnp.bfloat16)
    return (layer_out, kv_cache)


def solution(mesh):
    placed = (
        P("seq", None),
        P(),
        P("seq", "mp"),
        P(None, "seq", None),
        P("seq", "mp"),
        P("seq"),
        P("seq"),
    )
    return jax.shard_map(
        body,
        mesh=mesh,
        in_specs=placed,
        out_specs=(P("seq", "mp"), P("seq", "mp", None)),
        check_vma=False,
    )
```

```python
import math

import jax
import jax.numpy as jnp
from jax import lax
from jax.sharding import Mesh, PartitionSpec as P

W = 2048
PAGE = 128
SEGS = 32
MP = ("ylo", "x")


def from_behind(x, axis, by):
    peers = lax.axis_size(axis)
    pairs = [(i, i + by) for i in range(peers) if 0 <= i + by < peers]
    return lax.ppermute(x, axis, pairs)


def shift_round(x, axis, by):
    peers = lax.axis_size(axis)
    return lax.ppermute(x, axis, [(i, (i + by) % peers) for i in range(peers)])


def rotate_half(values, cosine, sine_table):
    half = values.shape[-1] // 2
    first_half = values[..., :half]
    second = values[..., half:]
    return jnp.concatenate(
        [first_half * cosine - second * sine_table, second * cosine + first_half * sine_table],
        axis=-1,
    )


def attend_piece(carry, piece, start, queries, query_first, query_start, block_rows):
    head_size = queries.shape[2]
    count = piece.shape[0]
    key_rows = piece[:, :head_size]
    value_rows = piece[:, head_size:]
    key_index = start + jnp.arange(count, dtype=jnp.int32)
    scale = 1.0 / math.sqrt(head_size)
    blocks = queries.shape[0] // block_rows

    def one_block(block, state):
        row_first = block * block_rows
        query_block = lax.dynamic_slice_in_dim(queries, row_first, block_rows, 0)
        query_index = query_first + row_first + jnp.arange(block_rows, dtype=jnp.int32)
        query_begin = lax.dynamic_slice_in_dim(query_start, row_first, block_rows, 0)
        lowest = jnp.maximum(query_begin[0], query_index[0] - W + 1)
        live = (start <= query_index[-1]) & (start + count - 1 >= lowest)

        def compute(inner):
            best, totals, accum = inner
            best_block = lax.dynamic_slice_in_dim(best, row_first, block_rows, 1)
            total_block = lax.dynamic_slice_in_dim(totals, row_first, block_rows, 1)
            accum_block = lax.dynamic_slice_in_dim(accum, row_first, block_rows, 1)
            scores = (
                jnp.einsum("qhd,kd->hqk", query_block, key_rows, preferred_element_type=jnp.float32)
                * scale
            )
            keep = (key_index[None, :] >= query_begin[:, None]) & (
                key_index[None, :] <= query_index[:, None]
            )
            keep = keep & (query_index[:, None] - key_index[None, :] < W)
            masked = jnp.where(keep[None], scores, -1e30)
            new_best = jnp.maximum(best_block, jnp.max(masked, axis=-1))
            weights = jnp.where(keep[None], jnp.exp(masked - new_best[..., None]), 0.0)
            factor = jnp.exp(best_block - new_best)
            new_total = total_block * factor + jnp.sum(weights, axis=-1)
            mixed = jnp.einsum(
                "hqk,kd->hqd",
                weights.astype(jnp.bfloat16),
                value_rows,
                preferred_element_type=jnp.float32,
            )
            new_accum = accum_block * factor[..., None] + mixed
            best = lax.dynamic_update_slice_in_dim(best, new_best, row_first, 1)
            totals = lax.dynamic_update_slice_in_dim(totals, new_total, row_first, 1)
            accum = lax.dynamic_update_slice_in_dim(accum, new_accum, row_first, 1)
            return (best, totals, accum)

        return lax.cond(live, compute, lambda inner: inner, state)

    return lax.fori_loop(0, blocks, one_block, carry)


def body(tokens_in, norm_gain, q_weight, kv_weight, out_weight, segment_ids, page_table):
    seq_count = lax.axis_size("seq")
    mp_count = lax.axis_size(MP)
    seq_index = lax.axis_index("seq")
    mp_index = lax.axis_index(MP)
    tok_rows = tokens_in.shape[0]
    kv_heads = kv_weight.shape[0]
    head_size = kv_weight.shape[2] // 2
    ratio = mp_count // kv_heads
    own_head = mp_index // ratio
    kv_own = lax.dynamic_index_in_dim(kv_weight, own_head, 0, keepdims=False)
    q_columns = q_weight.shape[1]
    w_inputs = lax.all_gather(
        jnp.concatenate([q_weight, kv_own], axis=1), "seq", axis=0, tiled=True
    )
    w_output = lax.all_gather(out_weight, "seq", axis=0, tiled=True)
    inputs = tokens_in.astype(jnp.float32)
    meansq = jnp.mean(inputs * inputs, axis=-1, keepdims=True)
    normed = (inputs * lax.rsqrt(meansq + 1e-05) * norm_gain).astype(jnp.bfloat16)
    token_first = seq_index * tok_rows
    global_index = token_first + jnp.arange(tok_rows, dtype=jnp.int32)
    seg_values = jnp.arange(SEGS, dtype=jnp.int32)
    seg_hist = jnp.sum((segment_ids[:, None] == seg_values[None, :]).astype(jnp.int32), axis=0)
    seg_total = lax.psum(seg_hist, "seq")
    seg_first = jnp.cumsum(seg_total) - seg_total
    query_start = jnp.sum(
        jnp.where(segment_ids[:, None] == seg_values[None, :], seg_first[None, :], 0), axis=1
    )
    positions = global_index - query_start
    half = head_size // 2
    freqs = jnp.exp(jnp.arange(half, dtype=jnp.float32) * (-2.0 * math.log(10000.0) / head_size))
    angles = positions.astype(jnp.float32)[:, None] * freqs[None, :]
    cosine = jnp.cos(angles)
    sine_table = jnp.sin(angles)
    local_heads = q_columns // head_size
    projected_all = jnp.dot(normed, w_inputs, preferred_element_type=jnp.float32)
    queries = projected_all[:, :q_columns].reshape(tok_rows, local_heads, head_size)
    queries = rotate_half(queries, cosine[:, None, :], sine_table[:, None, :]).astype(jnp.bfloat16)
    projected = projected_all[:, q_columns:]
    key_rows = rotate_half(projected[:, :head_size], cosine, sine_table).astype(jnp.bfloat16)
    value_rows = projected[:, head_size:].astype(jnp.bfloat16)
    keyval = jnp.concatenate([key_rows, value_rows], axis=1)
    block_rows = min(512, tok_rows)
    initial = (
        jnp.full((local_heads, tok_rows), -1e30, jnp.float32),
        jnp.zeros((local_heads, tok_rows), jnp.float32),
        jnp.zeros((local_heads, tok_rows, head_size), jnp.float32),
    )

    def fold_piece(carry, piece, start):
        return attend_piece(carry, piece, start, queries, token_first, query_start, block_rows)

    state = fold_piece(initial, keyval, token_first)
    earlier = from_behind(keyval, "seq", 1)
    state = fold_piece(state, earlier, token_first - tok_rows)
    best, totals, accum = state
    attended = (
        (accum / totals[..., None])
        .transpose(1, 0, 2)
        .reshape(tok_rows, local_heads * head_size)
        .astype(jnp.bfloat16)
    )
    rows_mp, cols_mp = (lax.axis_size(MP[0]), lax.axis_size(MP[1]))
    out_blocks = w_output.reshape(rows_mp, cols_mp, -1, w_output.shape[1])
    grouped = jnp.einsum(
        "tk,yxck->yxtc", attended, out_blocks, preferred_element_type=jnp.float32
    ).astype(jnp.bfloat16)
    grouped = lax.psum_scatter(grouped, MP[0], scatter_dimension=0, tiled=True)
    grouped = lax.psum_scatter(grouped, MP[1], scatter_dimension=1, tiled=True)
    layer_out = grouped.reshape(tok_rows, -1)
    pages_dev = tok_rows // PAGE
    share_width = 2 * head_size // ratio
    share_index = mp_index % ratio
    share = lax.dynamic_slice_in_dim(keyval, share_index * share_width, share_width, 1)
    page_blocks = share.reshape(pages_dev, PAGE, share_width).transpose(0, 2, 1)
    owners = page_table // pages_dev
    local_slot = page_table % pages_dev
    spread = min(seq_count, pages_dev)
    capacity = pages_dev // spread
    page_order = jnp.arange(pages_dev, dtype=jnp.int32)
    same_owner = (owners[:, None] == owners[None, :]) & (page_order[None, :] < page_order[:, None])
    ranking = jnp.sum(same_owner.astype(jnp.int32), axis=1)
    lanes_all = seq_count * capacity
    send_lane = ((owners - seq_index) % seq_count) * capacity + ranking
    select = jnp.arange(lanes_all, dtype=jnp.int32)[:, None] == send_lane[None, :]
    outgoing = jnp.einsum(
        "sp,pfk->sfk", select.astype(jnp.bfloat16), page_blocks, preferred_element_type=jnp.float32
    ).astype(jnp.bfloat16)
    labels = jnp.sum(jnp.where(select, (local_slot + 1)[None, :], 0), axis=1)
    label_rows = jnp.broadcast_to(labels.astype(jnp.bfloat16)[:, None, None], (lanes_all, 1, PAGE))
    payload = jnp.concatenate([outgoing, label_rows], axis=1)
    arrived = [payload[:capacity]]
    for offset in range(1, seq_count):
        lanes = slice(offset * capacity, (offset + 1) * capacity)
        arrived.append(shift_round(payload[lanes], "seq", offset))
    landed = jnp.concatenate(arrived, axis=0)
    incoming = landed[:, :share_width]
    tags = landed[:, share_width, 0].astype(jnp.int32)
    placement = (tags[None, :] == (page_order + 1)[:, None]).astype(jnp.bfloat16)
    kv_cache = jnp.einsum(
        "ps,sfk->pfk", placement, incoming, preferred_element_type=jnp.float32
    ).astype(jnp.bfloat16)
    return (layer_out, kv_cache)


def solution(mesh):
    seq_size, mp_size = (mesh.shape["seq"], mesh.shape["mp"])
    split = Mesh(mesh.devices.reshape(seq_size, 2, mp_size // 2), ("seq",) + MP)
    placed = (
        P("seq", None),
        P(),
        P("seq", MP),
        P(None, "seq", None),
        P("seq", MP),
        P("seq"),
        P("seq"),
    )
    return jax.shard_map(
        body,
        mesh=split,
        in_specs=placed,
        out_specs=(P("seq", MP), P("seq", MP, None)),
        check_vma=False,
    )
```

```python
import functools
import math

import jax
import jax.numpy as jnp
from jax import lax
from jax.experimental import pallas as pl
from jax.experimental.pallas import tpu as pltpu
from jax.sharding import PartitionSpec as P

W = 2048
PAGE = 128
SEGS = 32


def from_behind(x, axis, by):
    peers = lax.axis_size(axis)
    pairs = [(i, i + by) for i in range(peers) if 0 <= i + by < peers]
    return lax.ppermute(x, axis, pairs)


def shift_round(x, axis, by):
    peers = lax.axis_size(axis)
    return lax.ppermute(x, axis, [(i, (i + by) % peers) for i in range(peers)])


def rotate_half(values, cosine, sine_table):
    half = values.shape[-1] // 2
    first_half = values[..., :half]
    second = values[..., half:]
    return jnp.concatenate(
        [first_half * cosine - second * sine_table, second * cosine + first_half * sine_table],
        axis=-1,
    )


def flash_kernel(q_rows, tokens, first_ref, lowest_ref, q_ref, k_ref, v_ref, qs_ref, o_ref, m_sc, l_sc, acc_sc):
    block = pl.program_id(0)
    step = pl.program_id(1)
    rows = q_ref.shape[0]
    k_rows = k_ref.shape[0]
    head_size = q_ref.shape[1]

    @pl.when(step == 0)
    def _():
        m_sc[...] = jnp.full(m_sc.shape, -1e30, jnp.float32)
        l_sc[...] = jnp.zeros(l_sc.shape, jnp.float32)
        acc_sc[...] = jnp.zeros(acc_sc.shape, jnp.float32)

    token_first = first_ref[0]
    query_first = token_first + block * q_rows
    key_first = token_first - tokens + (block * q_rows // k_rows + step) * k_rows
    key_last = key_first + k_rows - 1
    live = (key_last >= lowest_ref[block]) & (key_first <= query_first + q_rows - 1)
    live = live & (query_first - key_last < W)

    @pl.when(live)
    def _():
        scores = lax.dot_general(
            q_ref[...], k_ref[...], (((1,), (1,)), ((), ())), preferred_element_type=jnp.float32
        ) * (1.0 / math.sqrt(head_size))
        key_index = key_first + lax.broadcasted_iota(jnp.int32, (rows, k_rows), 1)
        query_index = query_first + lax.broadcasted_iota(jnp.int32, (rows, k_rows), 0) % q_rows
        keep = (key_index >= qs_ref[...]) & (key_index <= query_index)
        keep = keep & (query_index - key_index < W)
        masked = jnp.where(keep, scores, -1e30)
        best = m_sc[...]
        new_best = jnp.maximum(best, jnp.max(masked, axis=1, keepdims=True))
        weights = jnp.where(keep, jnp.exp(masked - new_best), 0.0)
        factor = jnp.exp(best - new_best)
        l_sc[...] = l_sc[...] * factor + jnp.sum(weights, axis=1, keepdims=True)
        mixed = jnp.dot(weights.astype(jnp.bfloat16), v_ref[...], preferred_element_type=jnp.float32)
        acc_sc[...] = acc_sc[...] * factor + mixed
        m_sc[...] = new_best

    @pl.when(step == pl.num_programs(1) - 1)
    def _():
        o_ref[...] = (acc_sc[...] / l_sc[...]).astype(o_ref.dtype)


def flash_attention(queries, keys, values, query_start, token_first):
    tokens, heads, head_size = queries.shape
    q_rows = min(256, tokens)
    k_rows = 2 * q_rows
    blocks = tokens // q_rows
    steps = (W + q_rows) // k_rows + 1
    stacked = queries.reshape(blocks, q_rows, heads, head_size).transpose(0, 2, 1, 3)
    stacked = stacked.reshape(blocks * heads * q_rows, head_size)
    starts = jnp.broadcast_to(
        query_start.reshape(blocks, 1, q_rows), (blocks, heads, q_rows)
    ).reshape(blocks * heads * q_rows, 1)
    lowest = jnp.min(query_start.reshape(blocks, q_rows), axis=1)
    rows = heads * q_rows

    def kv_map(i, j, first, low):
        return (i * q_rows // k_rows + j, 0)

    out = pl.pallas_call(
        functools.partial(flash_kernel, q_rows, tokens),
        grid_spec=pltpu.PrefetchScalarGridSpec(
            num_scalar_prefetch=2,
            grid=(blocks, steps),
            in_specs=[
                pl.BlockSpec((rows, head_size), lambda i, j, first, low: (i, 0)),
                pl.BlockSpec((k_rows, head_size), kv_map),
                pl.BlockSpec((k_rows, head_size), kv_map),
                pl.BlockSpec((rows, 1), lambda i, j, first, low: (i, 0)),
            ],
            out_specs=pl.BlockSpec((rows, head_size), lambda i, j, first, low: (i, 0)),
            scratch_shapes=[
                pltpu.VMEM((rows, 1), jnp.float32),
                pltpu.VMEM((rows, 1), jnp.float32),
                pltpu.VMEM((rows, head_size), jnp.float32),
            ],
        ),
        out_shape=jax.ShapeDtypeStruct((blocks * rows, head_size), jnp.bfloat16),
        compiler_params=pltpu.CompilerParams(dimension_semantics=("arbitrary", "arbitrary")),
    )(token_first.reshape(1), lowest, stacked, keys, values, starts)
    return (
        out.reshape(blocks, heads, q_rows, head_size)
        .transpose(0, 2, 1, 3)
        .reshape(tokens, heads * head_size)
    )


def body(tokens_in, norm_gain, q_weight, kv_weight, out_weight, segment_ids, page_table):
    seq_count = lax.axis_size("seq")
    mp_count = lax.axis_size("mp")
    seq_index = lax.axis_index("seq")
    mp_index = lax.axis_index("mp")
    tok_rows = tokens_in.shape[0]
    kv_heads = kv_weight.shape[0]
    head_size = kv_weight.shape[2] // 2
    ratio = mp_count // kv_heads
    own_head = mp_index // ratio
    kv_own = lax.dynamic_index_in_dim(kv_weight, own_head, 0, keepdims=False)
    q_columns = q_weight.shape[1]
    w_inputs = lax.all_gather(
        jnp.concatenate([q_weight, kv_own], axis=1), "seq", axis=0, tiled=True
    )
    w_output = lax.all_gather(out_weight, "seq", axis=0, tiled=True)
    inputs = tokens_in.astype(jnp.float32)
    meansq = jnp.mean(inputs * inputs, axis=-1, keepdims=True)
    normed = (inputs * lax.rsqrt(meansq + 1e-05) * norm_gain).astype(jnp.bfloat16)
    token_first = seq_index * tok_rows
    global_index = token_first + jnp.arange(tok_rows, dtype=jnp.int32)
    seg_values = jnp.arange(SEGS, dtype=jnp.int32)
    seg_hist = jnp.sum((segment_ids[:, None] == seg_values[None, :]).astype(jnp.int32), axis=0)
    seg_total = lax.psum(seg_hist, "seq")
    seg_first = jnp.cumsum(seg_total) - seg_total
    query_start = jnp.sum(
        jnp.where(segment_ids[:, None] == seg_values[None, :], seg_first[None, :], 0), axis=1
    )
    positions = global_index - query_start
    half = head_size // 2
    freqs = jnp.exp(jnp.arange(half, dtype=jnp.float32) * (-2.0 * math.log(10000.0) / head_size))
    angles = positions.astype(jnp.float32)[:, None] * freqs[None, :]
    cosine = jnp.cos(angles)
    sine_table = jnp.sin(angles)
    local_heads = q_columns // head_size
    projected_all = jnp.dot(normed, w_inputs, preferred_element_type=jnp.float32)
    queries = projected_all[:, :q_columns].reshape(tok_rows, local_heads, head_size)
    queries = rotate_half(queries, cosine[:, None, :], sine_table[:, None, :]).astype(jnp.bfloat16)
    projected = projected_all[:, q_columns:]
    key_rows = rotate_half(projected[:, :head_size], cosine, sine_table).astype(jnp.bfloat16)
    value_rows = projected[:, head_size:].astype(jnp.bfloat16)
    keyval = jnp.concatenate([key_rows, value_rows], axis=1)
    earlier = from_behind(keyval, "seq", 1)
    window = jnp.concatenate([earlier, keyval], axis=0)
    attended = flash_attention(
        queries, window[:, :head_size], window[:, head_size:], query_start, token_first
    )
    partial_term = lax.dot_general(
        attended, w_output, (((1,), (1,)), ((), ())), preferred_element_type=jnp.float32
    )
    layer_out = lax.psum_scatter(
        partial_term.astype(jnp.bfloat16), "mp", scatter_dimension=1, tiled=True
    )
    pages_dev = tok_rows // PAGE
    share_width = 2 * head_size // ratio
    share_index = mp_index % ratio
    share = lax.dynamic_slice_in_dim(keyval, share_index * share_width, share_width, 1)
    page_blocks = share.reshape(pages_dev, PAGE, share_width).transpose(0, 2, 1)
    owners = page_table // pages_dev
    local_slot = page_table % pages_dev
    spread = min(seq_count, pages_dev)
    capacity = pages_dev // spread
    page_order = jnp.arange(pages_dev, dtype=jnp.int32)
    same_owner = (owners[:, None] == owners[None, :]) & (page_order[None, :] < page_order[:, None])
    ranking = jnp.sum(same_owner.astype(jnp.int32), axis=1)
    lanes_all = seq_count * capacity
    send_lane = ((owners - seq_index) % seq_count) * capacity + ranking
    select = jnp.arange(lanes_all, dtype=jnp.int32)[:, None] == send_lane[None, :]
    outgoing = jnp.einsum(
        "sp,pfk->sfk", select.astype(jnp.bfloat16), page_blocks, preferred_element_type=jnp.float32
    ).astype(jnp.bfloat16)
    labels = jnp.sum(jnp.where(select, (local_slot + 1)[None, :], 0), axis=1)
    label_rows = jnp.broadcast_to(labels.astype(jnp.bfloat16)[:, None, None], (lanes_all, 1, PAGE))
    payload = jnp.concatenate([outgoing, label_rows], axis=1)
    arrived = [payload[:capacity]]
    for offset in range(1, seq_count):
        lanes = slice(offset * capacity, (offset + 1) * capacity)
        arrived.append(shift_round(payload[lanes], "seq", offset))
    landed = jnp.concatenate(arrived, axis=0)
    incoming = landed[:, :share_width]
    tags = landed[:, share_width, 0].astype(jnp.int32)
    placement = (tags[None, :] == (page_order + 1)[:, None]).astype(jnp.bfloat16)
    kv_cache = jnp.einsum(
        "ps,sfk->pfk", placement, incoming, preferred_element_type=jnp.float32
    ).astype(jnp.bfloat16)
    return (layer_out, kv_cache)


def solution(mesh):
    placed = (
        P("seq", None),
        P(),
        P("seq", "mp"),
        P(None, "seq", None),
        P("seq", "mp"),
        P("seq"),
        P("seq"),
    )
    return jax.shard_map(
        body,
        mesh=mesh,
        in_specs=placed,
        out_specs=(P("seq", "mp"), P("seq", "mp", None)),
        check_vma=False,
    )
```

```python
import functools
import math

import jax
import jax.numpy as jnp
from jax import lax
from jax.experimental import pallas as pl
from jax.experimental.pallas import tpu as pltpu
from jax.sharding import PartitionSpec as P

W = 2048
PAGE = 128
SEGS = 32


def from_behind(x, axis, by):
    peers = lax.axis_size(axis)
    pairs = [(i, i + by) for i in range(peers) if 0 <= i + by < peers]
    return lax.ppermute(x, axis, pairs)


def shift_round(x, axis, by):
    peers = lax.axis_size(axis)
    return lax.ppermute(x, axis, [(i, (i + by) % peers) for i in range(peers)])


def rotate_half(values, cosine, sine_table):
    half = values.shape[-1] // 2
    first_half = values[..., :half]
    second = values[..., half:]
    return jnp.concatenate(
        [first_half * cosine - second * sine_table, second * cosine + first_half * sine_table],
        axis=-1,
    )


def flash_kernel(q_rows, tokens, first_ref, lowest_ref, highest_ref, q_ref, k_ref, v_ref, qs_ref, o_ref, m_sc, l_sc, acc_sc):
    block = pl.program_id(0)
    step = pl.program_id(1)
    rows = q_ref.shape[0]
    k_rows = k_ref.shape[0]

    @pl.when(step == 0)
    def _():
        m_sc[...] = jnp.full(m_sc.shape, -1e30, jnp.float32)
        l_sc[...] = jnp.zeros(l_sc.shape, jnp.float32)
        acc_sc[...] = jnp.zeros(acc_sc.shape, jnp.float32)

    token_first = first_ref[0]
    query_first = token_first + block * q_rows
    key_first = token_first - tokens + (block * q_rows // k_rows + step) * k_rows
    key_last = key_first + k_rows - 1
    live = (key_last >= lowest_ref[block]) & (key_first <= query_first + q_rows - 1)
    live = live & (query_first - key_last < W)

    full = (key_first >= highest_ref[block]) & (key_last <= query_first)
    full = full & (query_first + q_rows - 1 - key_first < W)

    def update(masked):
        best = m_sc[...]
        new_best = jnp.maximum(best, jnp.max(masked, axis=1, keepdims=True))
        weights = jnp.exp(masked - new_best)
        factor = jnp.exp(best - new_best)
        l_sc[...] = l_sc[...] * factor + jnp.sum(weights, axis=1, keepdims=True)
        mixed = jnp.dot(weights.astype(jnp.bfloat16), v_ref[...], preferred_element_type=jnp.float32)
        acc_sc[...] = acc_sc[...] * factor + mixed
        m_sc[...] = new_best

    def scores():
        return lax.dot_general(
            q_ref[...], k_ref[...], (((1,), (1,)), ((), ())), preferred_element_type=jnp.float32
        )

    @pl.when(live & full)
    def _():
        update(scores())

    @pl.when(live & jnp.logical_not(full))
    def _():
        key_index = key_first + lax.broadcasted_iota(jnp.int32, (rows, k_rows), 1)
        query_index = query_first + lax.broadcasted_iota(jnp.int32, (rows, k_rows), 0) % q_rows
        keep = (key_index >= qs_ref[...]) & (key_index <= query_index)
        keep = keep & (query_index - key_index < W)
        update(jnp.where(keep, scores(), -jnp.inf))

    @pl.when(step == pl.num_programs(1) - 1)
    def _():
        o_ref[...] = (acc_sc[...] / l_sc[...]).astype(o_ref.dtype)


def flash_attention(queries, keys, values, query_start, token_first):
    tokens, heads, head_size = queries.shape
    q_rows = min(256, tokens)
    k_rows = 2 * q_rows
    blocks = tokens // q_rows
    steps = (W + q_rows) // k_rows + 1
    scaled = queries * jnp.asarray(1.0 / math.sqrt(head_size), queries.dtype)
    stacked = scaled.reshape(blocks, q_rows, heads, head_size).transpose(0, 2, 1, 3)
    stacked = stacked.reshape(blocks * heads * q_rows, head_size)
    starts = jnp.broadcast_to(
        query_start.reshape(blocks, 1, q_rows), (blocks, heads, q_rows)
    ).reshape(blocks * heads * q_rows, 1)
    lowest = jnp.min(query_start.reshape(blocks, q_rows), axis=1)
    highest = jnp.max(query_start.reshape(blocks, q_rows), axis=1)
    rows = heads * q_rows

    def kv_map(i, j, first, low, high):
        return (i * q_rows // k_rows + j, 0)

    out = pl.pallas_call(
        functools.partial(flash_kernel, q_rows, tokens),
        grid_spec=pltpu.PrefetchScalarGridSpec(
            num_scalar_prefetch=3,
            grid=(blocks, steps),
            in_specs=[
                pl.BlockSpec((rows, head_size), lambda i, j, first, low, high: (i, 0)),
                pl.BlockSpec((k_rows, head_size), kv_map),
                pl.BlockSpec((k_rows, head_size), kv_map),
                pl.BlockSpec((rows, 1), lambda i, j, first, low, high: (i, 0)),
            ],
            out_specs=pl.BlockSpec((rows, head_size), lambda i, j, first, low, high: (i, 0)),
            scratch_shapes=[
                pltpu.VMEM((rows, 1), jnp.float32),
                pltpu.VMEM((rows, 1), jnp.float32),
                pltpu.VMEM((rows, head_size), jnp.float32),
            ],
        ),
        out_shape=jax.ShapeDtypeStruct((blocks * rows, head_size), jnp.bfloat16),
        compiler_params=pltpu.CompilerParams(dimension_semantics=("arbitrary", "arbitrary")),
    )(token_first.reshape(1), lowest, highest, stacked, keys, values, starts)
    return (
        out.reshape(blocks, heads, q_rows, head_size)
        .transpose(0, 2, 1, 3)
        .reshape(tokens, heads * head_size)
    )


def body(tokens_in, norm_gain, q_weight, kv_weight, out_weight, segment_ids, page_table):
    seq_count = lax.axis_size("seq")
    mp_count = lax.axis_size("mp")
    seq_index = lax.axis_index("seq")
    mp_index = lax.axis_index("mp")
    tok_rows = tokens_in.shape[0]
    kv_heads = kv_weight.shape[0]
    head_size = kv_weight.shape[2] // 2
    ratio = mp_count // kv_heads
    own_head = mp_index // ratio
    kv_own = lax.dynamic_index_in_dim(kv_weight, own_head, 0, keepdims=False)
    q_columns = q_weight.shape[1]
    w_inputs = lax.all_gather(
        jnp.concatenate([q_weight, kv_own], axis=1), "seq", axis=0, tiled=True
    )
    w_output = lax.all_gather(out_weight, "seq", axis=0, tiled=True)
    inputs = tokens_in.astype(jnp.float32)
    meansq = jnp.mean(inputs * inputs, axis=-1, keepdims=True)
    normed = (inputs * lax.rsqrt(meansq + 1e-05) * norm_gain).astype(jnp.bfloat16)
    token_first = seq_index * tok_rows
    global_index = token_first + jnp.arange(tok_rows, dtype=jnp.int32)
    seg_values = jnp.arange(SEGS, dtype=jnp.int32)
    seg_hist = jnp.sum((segment_ids[:, None] == seg_values[None, :]).astype(jnp.int32), axis=0)
    seg_total = lax.psum(seg_hist, "seq")
    seg_first = jnp.cumsum(seg_total) - seg_total
    query_start = jnp.sum(
        jnp.where(segment_ids[:, None] == seg_values[None, :], seg_first[None, :], 0), axis=1
    )
    positions = global_index - query_start
    half = head_size // 2
    freqs = jnp.exp(jnp.arange(half, dtype=jnp.float32) * (-2.0 * math.log(10000.0) / head_size))
    angles = positions.astype(jnp.float32)[:, None] * freqs[None, :]
    cosine = jnp.cos(angles)
    sine_table = jnp.sin(angles)
    local_heads = q_columns // head_size
    projected_all = jnp.dot(normed, w_inputs, preferred_element_type=jnp.float32)
    queries = projected_all[:, :q_columns].reshape(tok_rows, local_heads, head_size)
    queries = rotate_half(queries, cosine[:, None, :], sine_table[:, None, :]).astype(jnp.bfloat16)
    projected = projected_all[:, q_columns:]
    key_rows = rotate_half(projected[:, :head_size], cosine, sine_table).astype(jnp.bfloat16)
    value_rows = projected[:, head_size:].astype(jnp.bfloat16)
    keyval = jnp.concatenate([key_rows, value_rows], axis=1)
    earlier = from_behind(keyval, "seq", 1)
    window = jnp.concatenate([earlier, keyval], axis=0)
    attended = flash_attention(
        queries, window[:, :head_size], window[:, head_size:], query_start, token_first
    )
    partial_term = lax.dot_general(
        attended, w_output, (((1,), (1,)), ((), ())), preferred_element_type=jnp.float32
    )
    layer_out = lax.psum_scatter(
        partial_term.astype(jnp.bfloat16), "mp", scatter_dimension=1, tiled=True
    )
    pages_dev = tok_rows // PAGE
    share_width = 2 * head_size // ratio
    share_index = mp_index % ratio
    share = lax.dynamic_slice_in_dim(keyval, share_index * share_width, share_width, 1)
    page_blocks = share.reshape(pages_dev, PAGE, share_width).transpose(0, 2, 1)
    owners = page_table // pages_dev
    local_slot = page_table % pages_dev
    spread = min(seq_count, pages_dev)
    capacity = pages_dev // spread
    page_order = jnp.arange(pages_dev, dtype=jnp.int32)
    same_owner = (owners[:, None] == owners[None, :]) & (page_order[None, :] < page_order[:, None])
    ranking = jnp.sum(same_owner.astype(jnp.int32), axis=1)
    lanes_all = seq_count * capacity
    send_lane = ((owners - seq_index) % seq_count) * capacity + ranking
    select = jnp.arange(lanes_all, dtype=jnp.int32)[:, None] == send_lane[None, :]
    outgoing = jnp.einsum(
        "sp,pfk->sfk", select.astype(jnp.bfloat16), page_blocks, preferred_element_type=jnp.float32
    ).astype(jnp.bfloat16)
    labels = jnp.sum(jnp.where(select, (local_slot + 1)[None, :], 0), axis=1)
    label_rows = jnp.broadcast_to(labels.astype(jnp.bfloat16)[:, None, None], (lanes_all, 1, PAGE))
    payload = jnp.concatenate([outgoing, label_rows], axis=1)
    arrived = [payload[:capacity]]
    for offset in range(1, seq_count):
        lanes = slice(offset * capacity, (offset + 1) * capacity)
        arrived.append(shift_round(payload[lanes], "seq", offset))
    landed = jnp.concatenate(arrived, axis=0)
    incoming = landed[:, :share_width]
    tags = landed[:, share_width, 0].astype(jnp.int32)
    placement = (tags[None, :] == (page_order + 1)[:, None]).astype(jnp.bfloat16)
    kv_cache = jnp.einsum(
        "ps,sfk->pfk", placement, incoming, preferred_element_type=jnp.float32
    ).astype(jnp.bfloat16)
    return (layer_out, kv_cache)


def solution(mesh):
    placed = (
        P("seq", None),
        P(),
        P("seq", "mp"),
        P(None, "seq", None),
        P("seq", "mp"),
        P("seq"),
        P("seq"),
    )
    return jax.shard_map(
        body,
        mesh=mesh,
        in_specs=placed,
        out_specs=(P("seq", "mp"), P("seq", "mp", None)),
        check_vma=False,
    )
```

```python
import functools
import math

import jax
import jax.numpy as jnp
from jax import lax
from jax.experimental import pallas as pl
from jax.experimental.pallas import tpu as pltpu
from jax.sharding import PartitionSpec as P

W = 2048
PAGE = 128
SEGS = 32


def from_behind(x, axis, by):
    peers = lax.axis_size(axis)
    pairs = [(i, i + by) for i in range(peers) if 0 <= i + by < peers]
    return lax.ppermute(x, axis, pairs)


def shift_round(x, axis, by):
    peers = lax.axis_size(axis)
    return lax.ppermute(x, axis, [(i, (i + by) % peers) for i in range(peers)])


def rotate_half(values, cosine, sine_table):
    half = values.shape[-1] // 2
    first_half = values[..., :half]
    second = values[..., half:]
    return jnp.concatenate(
        [first_half * cosine - second * sine_table, second * cosine + first_half * sine_table],
        axis=-1,
    )


def flash_kernel(q_rows, tokens, first_block, first_ref, lowest_ref, q_ref, k_ref, v_ref, qs_ref, o_ref, m_sc, l_sc, acc_sc):
    block = pl.program_id(0) + first_block
    step = pl.program_id(1)
    rows = q_ref.shape[0]
    k_rows = k_ref.shape[0]
    head_size = q_ref.shape[1]

    @pl.when(step == 0)
    def _():
        m_sc[...] = jnp.full(m_sc.shape, -1e30, jnp.float32)
        l_sc[...] = jnp.zeros(l_sc.shape, jnp.float32)
        acc_sc[...] = jnp.zeros(acc_sc.shape, jnp.float32)

    token_first = first_ref[0]
    query_first = token_first + block * q_rows
    key_first = token_first - tokens + (block * q_rows // k_rows + step) * k_rows
    key_last = key_first + k_rows - 1
    live = (key_last >= lowest_ref[block]) & (key_first <= query_first + q_rows - 1)
    live = live & (query_first - key_last < W)

    @pl.when(live)
    def _():
        scores = lax.dot_general(
            q_ref[...], k_ref[...], (((1,), (1,)), ((), ())), preferred_element_type=jnp.float32
        ) * (1.0 / math.sqrt(head_size))
        key_index = key_first + lax.broadcasted_iota(jnp.int32, (rows, k_rows), 1)
        query_index = query_first + lax.broadcasted_iota(jnp.int32, (rows, k_rows), 0) % q_rows
        keep = (key_index >= qs_ref[...]) & (key_index <= query_index)
        keep = keep & (query_index - key_index < W)
        masked = jnp.where(keep, scores, -1e30)
        best = m_sc[...]
        new_best = jnp.maximum(best, jnp.max(masked, axis=1, keepdims=True))
        weights = jnp.where(keep, jnp.exp(masked - new_best), 0.0)
        factor = jnp.exp(best - new_best)
        l_sc[...] = l_sc[...] * factor + jnp.sum(weights, axis=1, keepdims=True)
        mixed = jnp.dot(weights.astype(jnp.bfloat16), v_ref[...], preferred_element_type=jnp.float32)
        acc_sc[...] = acc_sc[...] * factor + mixed
        m_sc[...] = new_best

    @pl.when(step == pl.num_programs(1) - 1)
    def _():
        o_ref[...] = (acc_sc[...] / l_sc[...]).astype(o_ref.dtype)


def flash_attention(queries, keys, values, query_start, token_first, first_block, count):
    tokens, heads, head_size = queries.shape
    q_rows = min(256, tokens)
    k_rows = 2 * q_rows
    blocks = tokens // q_rows
    steps = (W + q_rows) // k_rows + 1
    stacked = queries.reshape(blocks, q_rows, heads, head_size).transpose(0, 2, 1, 3)
    stacked = stacked.reshape(blocks * heads * q_rows, head_size)
    starts = jnp.broadcast_to(
        query_start.reshape(blocks, 1, q_rows), (blocks, heads, q_rows)
    ).reshape(blocks * heads * q_rows, 1)
    lowest = jnp.min(query_start.reshape(blocks, q_rows), axis=1)
    rows = heads * q_rows

    def kv_map(i, j, first, low):
        return ((i + first_block) * q_rows // k_rows + j, 0)

    out = pl.pallas_call(
        functools.partial(flash_kernel, q_rows, tokens, first_block),
        grid_spec=pltpu.PrefetchScalarGridSpec(
            num_scalar_prefetch=2,
            grid=(count, steps),
            in_specs=[
                pl.BlockSpec((rows, head_size), lambda i, j, first, low: (i + first_block, 0)),
                pl.BlockSpec((k_rows, head_size), kv_map),
                pl.BlockSpec((k_rows, head_size), kv_map),
                pl.BlockSpec((rows, 1), lambda i, j, first, low: (i + first_block, 0)),
            ],
            out_specs=pl.BlockSpec((rows, head_size), lambda i, j, first, low: (i, 0)),
            scratch_shapes=[
                pltpu.VMEM((rows, 1), jnp.float32),
                pltpu.VMEM((rows, 1), jnp.float32),
                pltpu.VMEM((rows, head_size), jnp.float32),
            ],
        ),
        out_shape=jax.ShapeDtypeStruct((count * rows, head_size), jnp.bfloat16),
        compiler_params=pltpu.CompilerParams(dimension_semantics=("arbitrary", "arbitrary")),
    )(token_first.reshape(1), lowest, stacked, keys, values, starts)
    return (
        out.reshape(count, heads, q_rows, head_size)
        .transpose(0, 2, 1, 3)
        .reshape(count * q_rows, heads * head_size)
    )


def body(tokens_in, norm_gain, q_weight, kv_weight, out_weight, segment_ids, page_table):
    seq_count = lax.axis_size("seq")
    mp_count = lax.axis_size("mp")
    seq_index = lax.axis_index("seq")
    mp_index = lax.axis_index("mp")
    tok_rows = tokens_in.shape[0]
    kv_heads = kv_weight.shape[0]
    head_size = kv_weight.shape[2] // 2
    ratio = mp_count // kv_heads
    own_head = mp_index // ratio
    kv_own = lax.dynamic_index_in_dim(kv_weight, own_head, 0, keepdims=False)
    q_columns = q_weight.shape[1]
    w_inputs = lax.all_gather(
        jnp.concatenate([q_weight, kv_own], axis=1), "seq", axis=0, tiled=True
    )
    w_output = lax.all_gather(out_weight, "seq", axis=0, tiled=True)
    inputs = tokens_in.astype(jnp.float32)
    meansq = jnp.mean(inputs * inputs, axis=-1, keepdims=True)
    normed = (inputs * lax.rsqrt(meansq + 1e-05) * norm_gain).astype(jnp.bfloat16)
    token_first = seq_index * tok_rows
    global_index = token_first + jnp.arange(tok_rows, dtype=jnp.int32)
    seg_values = jnp.arange(SEGS, dtype=jnp.int32)
    seg_hist = jnp.sum((segment_ids[:, None] == seg_values[None, :]).astype(jnp.int32), axis=0)
    seg_total = lax.psum(seg_hist, "seq")
    seg_first = jnp.cumsum(seg_total) - seg_total
    query_start = jnp.sum(
        jnp.where(segment_ids[:, None] == seg_values[None, :], seg_first[None, :], 0), axis=1
    )
    positions = global_index - query_start
    half = head_size // 2
    freqs = jnp.exp(jnp.arange(half, dtype=jnp.float32) * (-2.0 * math.log(10000.0) / head_size))
    angles = positions.astype(jnp.float32)[:, None] * freqs[None, :]
    cosine = jnp.cos(angles)
    sine_table = jnp.sin(angles)
    local_heads = q_columns // head_size
    projected_all = jnp.dot(normed, w_inputs, preferred_element_type=jnp.float32)
    queries = projected_all[:, :q_columns].reshape(tok_rows, local_heads, head_size)
    queries = rotate_half(queries, cosine[:, None, :], sine_table[:, None, :]).astype(jnp.bfloat16)
    projected = projected_all[:, q_columns:]
    key_rows = rotate_half(projected[:, :head_size], cosine, sine_table).astype(jnp.bfloat16)
    value_rows = projected[:, head_size:].astype(jnp.bfloat16)
    keyval = jnp.concatenate([key_rows, value_rows], axis=1)
    earlier = from_behind(keyval, "seq", 1)
    window = jnp.concatenate([earlier, keyval], axis=0)
    halves = 2
    blocks_all = tok_rows // min(256, tok_rows)
    outputs = []
    for part in range(halves):
        attended = flash_attention(
            queries,
            window[:, :head_size],
            window[:, head_size:],
            query_start,
            token_first,
            part * blocks_all // halves,
            blocks_all // halves,
        )
        partial_term = lax.dot_general(
            attended, w_output, (((1,), (1,)), ((), ())), preferred_element_type=jnp.float32
        )
        outputs.append(
            lax.psum_scatter(partial_term.astype(jnp.bfloat16), "mp", scatter_dimension=1, tiled=True)
        )
    layer_out = jnp.concatenate(outputs, axis=0)
    pages_dev = tok_rows // PAGE
    share_width = 2 * head_size // ratio
    share_index = mp_index % ratio
    share = lax.dynamic_slice_in_dim(keyval, share_index * share_width, share_width, 1)
    page_blocks = share.reshape(pages_dev, PAGE, share_width).transpose(0, 2, 1)
    owners = page_table // pages_dev
    local_slot = page_table % pages_dev
    spread = min(seq_count, pages_dev)
    capacity = pages_dev // spread
    page_order = jnp.arange(pages_dev, dtype=jnp.int32)
    same_owner = (owners[:, None] == owners[None, :]) & (page_order[None, :] < page_order[:, None])
    ranking = jnp.sum(same_owner.astype(jnp.int32), axis=1)
    lanes_all = seq_count * capacity
    send_lane = ((owners - seq_index) % seq_count) * capacity + ranking
    select = jnp.arange(lanes_all, dtype=jnp.int32)[:, None] == send_lane[None, :]
    outgoing = jnp.einsum(
        "sp,pfk->sfk", select.astype(jnp.bfloat16), page_blocks, preferred_element_type=jnp.float32
    ).astype(jnp.bfloat16)
    labels = jnp.sum(jnp.where(select, (local_slot + 1)[None, :], 0), axis=1)
    label_rows = jnp.broadcast_to(labels.astype(jnp.bfloat16)[:, None, None], (lanes_all, 1, PAGE))
    payload = jnp.concatenate([outgoing, label_rows], axis=1)
    arrived = [payload[:capacity]]
    for offset in range(1, seq_count):
        lanes = slice(offset * capacity, (offset + 1) * capacity)
        arrived.append(shift_round(payload[lanes], "seq", offset))
    landed = jnp.concatenate(arrived, axis=0)
    incoming = landed[:, :share_width]
    tags = landed[:, share_width, 0].astype(jnp.int32)
    placement = (tags[None, :] == (page_order + 1)[:, None]).astype(jnp.bfloat16)
    kv_cache = jnp.einsum(
        "ps,sfk->pfk", placement, incoming, preferred_element_type=jnp.float32
    ).astype(jnp.bfloat16)
    return (layer_out, kv_cache)


def solution(mesh):
    placed = (
        P("seq", None),
        P(),
        P("seq", "mp"),
        P(None, "seq", None),
        P("seq", "mp"),
        P("seq"),
        P("seq"),
    )
    return jax.shard_map(
        body,
        mesh=mesh,
        in_specs=placed,
        out_specs=(P("seq", "mp"), P("seq", "mp", None)),
        check_vma=False,
    )
```

```python
import functools
import math

import jax
import jax.numpy as jnp
from jax import lax
from jax.experimental import pallas as pl
from jax.experimental.pallas import tpu as pltpu
from jax.sharding import PartitionSpec as P

W = 2048
PAGE = 128
SEGS = 32


def from_behind(x, axis, by):
    peers = lax.axis_size(axis)
    pairs = [(i, i + by) for i in range(peers) if 0 <= i + by < peers]
    return lax.ppermute(x, axis, pairs)


def shift_round(x, axis, by):
    peers = lax.axis_size(axis)
    return lax.ppermute(x, axis, [(i, (i + by) % peers) for i in range(peers)])


def rotate_half(values, cosine, sine_table):
    half = values.shape[-1] // 2
    first_half = values[..., :half]
    second = values[..., half:]
    return jnp.concatenate(
        [first_half * cosine - second * sine_table, second * cosine + first_half * sine_table],
        axis=-1,
    )


def flash_kernel(q_rows, tokens, first_ref, lowest_ref, q_ref, k_ref, v_ref, qs_ref, o_ref, m_sc, l_sc, acc_sc):
    block = pl.program_id(0) + first_ref[1]
    step = pl.program_id(1)
    rows = q_ref.shape[0]
    k_rows = k_ref.shape[0]
    head_size = q_ref.shape[1]

    @pl.when(step == 0)
    def _():
        m_sc[...] = jnp.full(m_sc.shape, -1e30, jnp.float32)
        l_sc[...] = jnp.zeros(l_sc.shape, jnp.float32)
        acc_sc[...] = jnp.zeros(acc_sc.shape, jnp.float32)

    token_first = first_ref[0]
    query_first = token_first + block * q_rows
    key_first = token_first - tokens + (block * q_rows // k_rows + step) * k_rows
    key_last = key_first + k_rows - 1
    live = (key_last >= lowest_ref[block]) & (key_first <= query_first + q_rows - 1)
    live = live & (query_first - key_last < W)

    @pl.when(live)
    def _():
        scores = lax.dot_general(
            q_ref[...], k_ref[...], (((1,), (1,)), ((), ())), preferred_element_type=jnp.float32
        ) * (1.0 / math.sqrt(head_size))
        key_index = key_first + lax.broadcasted_iota(jnp.int32, (rows, k_rows), 1)
        query_index = query_first + lax.broadcasted_iota(jnp.int32, (rows, k_rows), 0) % q_rows
        keep = (key_index >= qs_ref[...]) & (key_index <= query_index)
        keep = keep & (query_index - key_index < W)
        masked = jnp.where(keep, scores, -1e30)
        best = m_sc[...]
        new_best = jnp.maximum(best, jnp.max(masked, axis=1, keepdims=True))
        weights = jnp.where(keep, jnp.exp(masked - new_best), 0.0)
        factor = jnp.exp(best - new_best)
        l_sc[...] = l_sc[...] * factor + jnp.sum(weights, axis=1, keepdims=True)
        mixed = jnp.dot(weights.astype(jnp.bfloat16), v_ref[...], preferred_element_type=jnp.float32)
        acc_sc[...] = acc_sc[...] * factor + mixed
        m_sc[...] = new_best

    @pl.when(step == pl.num_programs(1) - 1)
    def _():
        o_ref[...] = (acc_sc[...] / l_sc[...]).astype(o_ref.dtype)


def flash_attention(queries, keys, values, query_start, token_first, first_block, count):
    tokens, heads, head_size = queries.shape
    q_rows = min(256, tokens)
    k_rows = 2 * q_rows
    blocks = tokens // q_rows
    steps = (W + q_rows) // k_rows + 1
    stacked = queries.reshape(blocks, q_rows, heads, head_size).transpose(0, 2, 1, 3)
    stacked = stacked.reshape(blocks * heads * q_rows, head_size)
    starts = jnp.broadcast_to(
        query_start.reshape(blocks, 1, q_rows), (blocks, heads, q_rows)
    ).reshape(blocks * heads * q_rows, 1)
    lowest = jnp.min(query_start.reshape(blocks, q_rows), axis=1)
    rows = heads * q_rows

    def kv_map(i, j, first, low):
        return ((i + first[1]) * q_rows // k_rows + j, 0)

    out = pl.pallas_call(
        functools.partial(flash_kernel, q_rows, tokens),
        grid_spec=pltpu.PrefetchScalarGridSpec(
            num_scalar_prefetch=2,
            grid=(count, steps),
            in_specs=[
                pl.BlockSpec((rows, head_size), lambda i, j, first, low: (i + first[1], 0)),
                pl.BlockSpec((k_rows, head_size), kv_map),
                pl.BlockSpec((k_rows, head_size), kv_map),
                pl.BlockSpec((rows, 1), lambda i, j, first, low: (i + first[1], 0)),
            ],
            out_specs=pl.BlockSpec((rows, head_size), lambda i, j, first, low: (i, 0)),
            scratch_shapes=[
                pltpu.VMEM((rows, 1), jnp.float32),
                pltpu.VMEM((rows, 1), jnp.float32),
                pltpu.VMEM((rows, head_size), jnp.float32),
            ],
        ),
        out_shape=jax.ShapeDtypeStruct((count * rows, head_size), jnp.bfloat16),
        compiler_params=pltpu.CompilerParams(dimension_semantics=("arbitrary", "arbitrary")),
    )(jnp.stack([token_first, jnp.int32(first_block)]), lowest, stacked, keys, values, starts)
    return (
        out.reshape(count, heads, q_rows, head_size)
        .transpose(0, 2, 1, 3)
        .reshape(count * q_rows, heads * head_size)
    )


def body(tokens_in, norm_gain, q_weight, kv_weight, out_weight, segment_ids, page_table):
    seq_count = lax.axis_size("seq")
    mp_count = lax.axis_size("mp")
    seq_index = lax.axis_index("seq")
    mp_index = lax.axis_index("mp")
    tok_rows = tokens_in.shape[0]
    kv_heads = kv_weight.shape[0]
    head_size = kv_weight.shape[2] // 2
    ratio = mp_count // kv_heads
    own_head = mp_index // ratio
    kv_own = lax.dynamic_index_in_dim(kv_weight, own_head, 0, keepdims=False)
    q_columns = q_weight.shape[1]
    w_inputs = lax.all_gather(
        jnp.concatenate([q_weight, kv_own], axis=1), "seq", axis=0, tiled=True
    )
    w_output = lax.all_gather(out_weight, "seq", axis=0, tiled=True)
    inputs = tokens_in.astype(jnp.float32)
    meansq = jnp.mean(inputs * inputs, axis=-1, keepdims=True)
    normed = (inputs * lax.rsqrt(meansq + 1e-05) * norm_gain).astype(jnp.bfloat16)
    token_first = seq_index * tok_rows
    global_index = token_first + jnp.arange(tok_rows, dtype=jnp.int32)
    seg_values = jnp.arange(SEGS, dtype=jnp.int32)
    seg_hist = jnp.sum((segment_ids[:, None] == seg_values[None, :]).astype(jnp.int32), axis=0)
    seg_total = lax.psum(seg_hist, "seq")
    seg_first = jnp.cumsum(seg_total) - seg_total
    query_start = jnp.sum(
        jnp.where(segment_ids[:, None] == seg_values[None, :], seg_first[None, :], 0), axis=1
    )
    positions = global_index - query_start
    half = head_size // 2
    freqs = jnp.exp(jnp.arange(half, dtype=jnp.float32) * (-2.0 * math.log(10000.0) / head_size))
    angles = positions.astype(jnp.float32)[:, None] * freqs[None, :]
    cosine = jnp.cos(angles)
    sine_table = jnp.sin(angles)
    local_heads = q_columns // head_size
    projected_all = jnp.dot(normed, w_inputs, preferred_element_type=jnp.float32)
    queries = projected_all[:, :q_columns].reshape(tok_rows, local_heads, head_size)
    queries = rotate_half(queries, cosine[:, None, :], sine_table[:, None, :]).astype(jnp.bfloat16)
    projected = projected_all[:, q_columns:]
    key_rows = rotate_half(projected[:, :head_size], cosine, sine_table).astype(jnp.bfloat16)
    value_rows = projected[:, head_size:].astype(jnp.bfloat16)
    keyval = jnp.concatenate([key_rows, value_rows], axis=1)
    earlier = from_behind(keyval, "seq", 1)
    window = jnp.concatenate([earlier, keyval], axis=0)
    halves = 4
    blocks_all = tok_rows // min(256, tok_rows)
    outputs = []
    for part in range(halves):
        attended = flash_attention(
            queries,
            window[:, :head_size],
            window[:, head_size:],
            query_start,
            token_first,
            part * blocks_all // halves,
            blocks_all // halves,
        )
        partial_term = lax.dot_general(
            attended, w_output, (((1,), (1,)), ((), ())), preferred_element_type=jnp.float32
        )
        outputs.append(
            lax.psum_scatter(partial_term.astype(jnp.bfloat16), "mp", scatter_dimension=1, tiled=True)
        )
    layer_out = jnp.concatenate(outputs, axis=0)
    pages_dev = tok_rows // PAGE
    share_width = 2 * head_size // ratio
    share_index = mp_index % ratio
    share = lax.dynamic_slice_in_dim(keyval, share_index * share_width, share_width, 1)
    page_blocks = share.reshape(pages_dev, PAGE, share_width).transpose(0, 2, 1)
    owners = page_table // pages_dev
    local_slot = page_table % pages_dev
    spread = min(seq_count, pages_dev)
    capacity = pages_dev // spread
    page_order = jnp.arange(pages_dev, dtype=jnp.int32)
    same_owner = (owners[:, None] == owners[None, :]) & (page_order[None, :] < page_order[:, None])
    ranking = jnp.sum(same_owner.astype(jnp.int32), axis=1)
    lanes_all = seq_count * capacity
    send_lane = ((owners - seq_index) % seq_count) * capacity + ranking
    select = jnp.arange(lanes_all, dtype=jnp.int32)[:, None] == send_lane[None, :]
    outgoing = jnp.einsum(
        "sp,pfk->sfk", select.astype(jnp.bfloat16), page_blocks, preferred_element_type=jnp.float32
    ).astype(jnp.bfloat16)
    labels = jnp.sum(jnp.where(select, (local_slot + 1)[None, :], 0), axis=1)
    label_rows = jnp.broadcast_to(labels.astype(jnp.bfloat16)[:, None, None], (lanes_all, 1, PAGE))
    payload = jnp.concatenate([outgoing, label_rows], axis=1)
    arrived = [payload[:capacity]]
    for offset in range(1, seq_count):
        lanes = slice(offset * capacity, (offset + 1) * capacity)
        arrived.append(shift_round(payload[lanes], "seq", offset))
    landed = jnp.concatenate(arrived, axis=0)
    incoming = landed[:, :share_width]
    tags = landed[:, share_width, 0].astype(jnp.int32)
    placement = (tags[None, :] == (page_order + 1)[:, None]).astype(jnp.bfloat16)
    kv_cache = jnp.einsum(
        "ps,sfk->pfk", placement, incoming, preferred_element_type=jnp.float32
    ).astype(jnp.bfloat16)
    return (layer_out, kv_cache)


def solution(mesh):
    placed = (
        P("seq", None),
        P(),
        P("seq", "mp"),
        P(None, "seq", None),
        P("seq", "mp"),
        P("seq"),
        P("seq"),
    )
    return jax.shard_map(
        body,
        mesh=mesh,
        in_specs=placed,
        out_specs=(P("seq", "mp"), P("seq", "mp", None)),
        check_vma=False,
    )
```

```python
import functools
import math

import jax
import jax.numpy as jnp
from jax import lax
from jax.experimental import pallas as pl
from jax.experimental.pallas import tpu as pltpu
from jax.sharding import PartitionSpec as P

W = 2048
PAGE = 128
SEGS = 32


def from_behind(x, axis, by):
    peers = lax.axis_size(axis)
    pairs = [(i, i + by) for i in range(peers) if 0 <= i + by < peers]
    return lax.ppermute(x, axis, pairs)


def shift_round(x, axis, by):
    peers = lax.axis_size(axis)
    return lax.ppermute(x, axis, [(i, (i + by) % peers) for i in range(peers)])


def rotate_half(values, cosine, sine_table):
    half = values.shape[-1] // 2
    first_half = values[..., :half]
    second = values[..., half:]
    return jnp.concatenate(
        [first_half * cosine - second * sine_table, second * cosine + first_half * sine_table],
        axis=-1,
    )


def flash_kernel(q_rows, tokens, first_block, first_ref, lowest_ref, q_ref, k_ref, v_ref, qs_ref, o_ref, m_sc, l_sc, acc_sc):
    block = pl.program_id(0) + first_block
    step = pl.program_id(1)
    rows = q_ref.shape[0]
    k_rows = k_ref.shape[0]
    head_size = q_ref.shape[1]

    @pl.when(step == 0)
    def _():
        m_sc[...] = jnp.full(m_sc.shape, -1e30, jnp.float32)
        l_sc[...] = jnp.zeros(l_sc.shape, jnp.float32)
        acc_sc[...] = jnp.zeros(acc_sc.shape, jnp.float32)

    token_first = first_ref[0]
    query_first = token_first + block * q_rows
    key_first = token_first - tokens + (block * q_rows // k_rows + step) * k_rows
    key_last = key_first + k_rows - 1
    live = (key_last >= lowest_ref[block]) & (key_first <= query_first + q_rows - 1)
    live = live & (query_first - key_last < W)

    @pl.when(live)
    def _():
        scores = lax.dot_general(
            q_ref[...], k_ref[...], (((1,), (1,)), ((), ())), preferred_element_type=jnp.float32
        ) * (1.0 / math.sqrt(head_size))
        key_index = key_first + lax.broadcasted_iota(jnp.int32, (rows, k_rows), 1)
        query_index = query_first + lax.broadcasted_iota(jnp.int32, (rows, k_rows), 0) % q_rows
        keep = (key_index >= qs_ref[...]) & (key_index <= query_index)
        keep = keep & (query_index - key_index < W)
        masked = jnp.where(keep, scores, -1e30)
        best = m_sc[...]
        new_best = jnp.maximum(best, jnp.max(masked, axis=1, keepdims=True))
        weights = jnp.where(keep, jnp.exp(masked - new_best), 0.0)
        factor = jnp.exp(best - new_best)
        l_sc[...] = l_sc[...] * factor + jnp.sum(weights, axis=1, keepdims=True)
        mixed = jnp.dot(weights.astype(jnp.bfloat16), v_ref[...], preferred_element_type=jnp.float32)
        acc_sc[...] = acc_sc[...] * factor + mixed
        m_sc[...] = new_best

    @pl.when(step == pl.num_programs(1) - 1)
    def _():
        o_ref[...] = (acc_sc[...] / l_sc[...]).astype(o_ref.dtype)


def flash_attention(queries, keys, values, query_start, token_first, first_block, count):
    tokens, heads, head_size = queries.shape
    q_rows = min(256, tokens)
    k_rows = 2 * q_rows
    blocks = tokens // q_rows
    steps = (W + q_rows) // k_rows + 1
    stacked = queries.reshape(blocks, q_rows, heads, head_size).transpose(0, 2, 1, 3)
    stacked = stacked.reshape(blocks * heads * q_rows, head_size)
    starts = jnp.broadcast_to(
        query_start.reshape(blocks, 1, q_rows), (blocks, heads, q_rows)
    ).reshape(blocks * heads * q_rows, 1)
    lowest = jnp.min(query_start.reshape(blocks, q_rows), axis=1)
    rows = heads * q_rows

    def kv_map(i, j, first, low):
        return ((i + first_block) * q_rows // k_rows + j, 0)

    out = pl.pallas_call(
        functools.partial(flash_kernel, q_rows, tokens, first_block),
        grid_spec=pltpu.PrefetchScalarGridSpec(
            num_scalar_prefetch=2,
            grid=(count, steps),
            in_specs=[
                pl.BlockSpec((rows, head_size), lambda i, j, first, low: (i + first_block, 0)),
                pl.BlockSpec((k_rows, head_size), kv_map),
                pl.BlockSpec((k_rows, head_size), kv_map),
                pl.BlockSpec((rows, 1), lambda i, j, first, low: (i + first_block, 0)),
            ],
            out_specs=pl.BlockSpec((rows, head_size), lambda i, j, first, low: (i, 0)),
            scratch_shapes=[
                pltpu.VMEM((rows, 1), jnp.float32),
                pltpu.VMEM((rows, 1), jnp.float32),
                pltpu.VMEM((rows, head_size), jnp.float32),
            ],
        ),
        out_shape=jax.ShapeDtypeStruct((count * rows, head_size), jnp.bfloat16),
        compiler_params=pltpu.CompilerParams(dimension_semantics=("arbitrary", "arbitrary")),
    )(token_first.reshape(1), lowest, stacked, keys, values, starts)
    return (
        out.reshape(count, heads, q_rows, head_size)
        .transpose(0, 2, 1, 3)
        .reshape(count * q_rows, heads * head_size)
    )


def body(tokens_in, norm_gain, q_weight, kv_weight, out_weight, segment_ids, page_table):
    seq_count = lax.axis_size("seq")
    mp_count = lax.axis_size("mp")
    seq_index = lax.axis_index("seq")
    mp_index = lax.axis_index("mp")
    tok_rows = tokens_in.shape[0]
    kv_heads = kv_weight.shape[0]
    head_size = kv_weight.shape[2] // 2
    ratio = mp_count // kv_heads
    own_head = mp_index // ratio
    kv_own = lax.dynamic_index_in_dim(kv_weight, own_head, 0, keepdims=False)
    q_columns = q_weight.shape[1]
    w_inputs = lax.all_gather(
        jnp.concatenate([q_weight, kv_own], axis=1), "seq", axis=0, tiled=True
    )
    w_output = lax.all_gather(out_weight, "seq", axis=0, tiled=True)
    inputs = tokens_in.astype(jnp.float32)
    meansq = jnp.mean(inputs * inputs, axis=-1, keepdims=True)
    normed = (inputs * lax.rsqrt(meansq + 1e-05) * norm_gain).astype(jnp.bfloat16)
    token_first = seq_index * tok_rows
    global_index = token_first + jnp.arange(tok_rows, dtype=jnp.int32)
    seg_values = jnp.arange(SEGS, dtype=jnp.int32)
    seg_hist = jnp.sum((segment_ids[:, None] == seg_values[None, :]).astype(jnp.int32), axis=0)
    seg_total = lax.psum(seg_hist, "seq")
    seg_first = jnp.cumsum(seg_total) - seg_total
    query_start = jnp.sum(
        jnp.where(segment_ids[:, None] == seg_values[None, :], seg_first[None, :], 0), axis=1
    )
    positions = global_index - query_start
    half = head_size // 2
    freqs = jnp.exp(jnp.arange(half, dtype=jnp.float32) * (-2.0 * math.log(10000.0) / head_size))
    angles = positions.astype(jnp.float32)[:, None] * freqs[None, :]
    cosine = jnp.cos(angles)
    sine_table = jnp.sin(angles)
    local_heads = q_columns // head_size
    projected_all = jnp.dot(normed, w_inputs, preferred_element_type=jnp.float32)
    queries = projected_all[:, :q_columns].reshape(tok_rows, local_heads, head_size)
    queries = rotate_half(queries, cosine[:, None, :], sine_table[:, None, :]).astype(jnp.bfloat16)
    projected = projected_all[:, q_columns:]
    key_rows = rotate_half(projected[:, :head_size], cosine, sine_table).astype(jnp.bfloat16)
    value_rows = projected[:, head_size:].astype(jnp.bfloat16)
    keyval = jnp.concatenate([key_rows, value_rows], axis=1)
    earlier = from_behind(keyval, "seq", 1)
    window = jnp.concatenate([earlier, keyval], axis=0)
    halves = 2
    out_groups = w_output.reshape(mp_count, -1, w_output.shape[1])
    blocks_all = tok_rows // min(256, tok_rows)
    outputs = []
    for part in range(halves):
        attended = flash_attention(
            queries,
            window[:, :head_size],
            window[:, head_size:],
            query_start,
            token_first,
            part * blocks_all // halves,
            blocks_all // halves,
        )
        partial_term = jnp.einsum(
            "tk,dck->dtc", attended, out_groups, preferred_element_type=jnp.float32
        )
        outputs.append(
            lax.psum_scatter(partial_term.astype(jnp.bfloat16), "mp", scatter_dimension=0, tiled=True)
        )
    layer_out = jnp.concatenate(outputs, axis=1)[0]
    pages_dev = tok_rows // PAGE
    share_width = 2 * head_size // ratio
    share_index = mp_index % ratio
    share = lax.dynamic_slice_in_dim(keyval, share_index * share_width, share_width, 1)
    page_blocks = share.reshape(pages_dev, PAGE, share_width).transpose(0, 2, 1)
    owners = page_table // pages_dev
    local_slot = page_table % pages_dev
    spread = min(seq_count, pages_dev)
    capacity = pages_dev // spread
    page_order = jnp.arange(pages_dev, dtype=jnp.int32)
    same_owner = (owners[:, None] == owners[None, :]) & (page_order[None, :] < page_order[:, None])
    ranking = jnp.sum(same_owner.astype(jnp.int32), axis=1)
    lanes_all = seq_count * capacity
    send_lane = ((owners - seq_index) % seq_count) * capacity + ranking
    select = jnp.arange(lanes_all, dtype=jnp.int32)[:, None] == send_lane[None, :]
    outgoing = jnp.einsum(
        "sp,pfk->sfk", select.astype(jnp.bfloat16), page_blocks, preferred_element_type=jnp.float32
    ).astype(jnp.bfloat16)
    labels = jnp.sum(jnp.where(select, (local_slot + 1)[None, :], 0), axis=1)
    label_rows = jnp.broadcast_to(labels.astype(jnp.bfloat16)[:, None, None], (lanes_all, 1, PAGE))
    payload = jnp.concatenate([outgoing, label_rows], axis=1)
    arrived = [payload[:capacity]]
    for offset in range(1, seq_count):
        lanes = slice(offset * capacity, (offset + 1) * capacity)
        arrived.append(shift_round(payload[lanes], "seq", offset))
    landed = jnp.concatenate(arrived, axis=0)
    incoming = landed[:, :share_width]
    tags = landed[:, share_width, 0].astype(jnp.int32)
    placement = (tags[None, :] == (page_order + 1)[:, None]).astype(jnp.bfloat16)
    kv_cache = jnp.einsum(
        "ps,sfk->pfk", placement, incoming, preferred_element_type=jnp.float32
    ).astype(jnp.bfloat16)
    return (layer_out, kv_cache)


def solution(mesh):
    placed = (
        P("seq", None),
        P(),
        P("seq", "mp"),
        P(None, "seq", None),
        P("seq", "mp"),
        P("seq"),
        P("seq"),
    )
    return jax.shard_map(
        body,
        mesh=mesh,
        in_specs=placed,
        out_specs=(P("seq", "mp"), P("seq", "mp", None)),
        check_vma=False,
    )
```

```python
import functools
import math

import jax
import jax.numpy as jnp
from jax import lax
from jax.experimental import pallas as pl
from jax.experimental.pallas import tpu as pltpu
from jax.sharding import PartitionSpec as P

W = 2048
PAGE = 128
SEGS = 32


def from_behind(x, axis, by):
    peers = lax.axis_size(axis)
    pairs = [(i, i + by) for i in range(peers) if 0 <= i + by < peers]
    return lax.ppermute(x, axis, pairs)


def shift_round(x, axis, by):
    peers = lax.axis_size(axis)
    return lax.ppermute(x, axis, [(i, (i + by) % peers) for i in range(peers)])


def rotate_half(values, cosine, sine_table):
    half = values.shape[-1] // 2
    first_half = values[..., :half]
    second = values[..., half:]
    return jnp.concatenate(
        [first_half * cosine - second * sine_table, second * cosine + first_half * sine_table],
        axis=-1,
    )


def flash_kernel(q_rows, tokens, first_block, first_ref, lowest_ref, q_ref, k_ref, v_ref, qs_ref, o_ref, m_sc, l_sc, acc_sc):
    block = pl.program_id(0) + first_block
    step = pl.program_id(1)
    rows = q_ref.shape[0]
    k_rows = k_ref.shape[0]
    head_size = q_ref.shape[1]

    @pl.when(step == 0)
    def _():
        m_sc[...] = jnp.full(m_sc.shape, -1e30, jnp.float32)
        l_sc[...] = jnp.zeros(l_sc.shape, jnp.float32)
        acc_sc[...] = jnp.zeros(acc_sc.shape, jnp.float32)

    token_first = first_ref[0]
    query_first = token_first + block * q_rows
    key_first = token_first - tokens + (block * q_rows // k_rows + step) * k_rows
    key_last = key_first + k_rows - 1
    live = (key_last >= lowest_ref[block]) & (key_first <= query_first + q_rows - 1)
    live = live & (query_first - key_last < W)

    @pl.when(live)
    def _():
        scores = lax.dot_general(
            q_ref[...], k_ref[...], (((1,), (1,)), ((), ())), preferred_element_type=jnp.float32
        ) * (1.0 / math.sqrt(head_size))
        key_index = key_first + lax.broadcasted_iota(jnp.int32, (rows, k_rows), 1)
        query_index = query_first + lax.broadcasted_iota(jnp.int32, (rows, k_rows), 0) % q_rows
        keep = (key_index >= qs_ref[...]) & (key_index <= query_index)
        keep = keep & (query_index - key_index < W)
        masked = jnp.where(keep, scores, -1e30)
        best = m_sc[...]
        new_best = jnp.maximum(best, jnp.max(masked, axis=1, keepdims=True))
        weights = jnp.where(keep, jnp.exp(masked - new_best), 0.0)
        factor = jnp.exp(best - new_best)
        l_sc[...] = l_sc[...] * factor + jnp.sum(weights, axis=1, keepdims=True)
        mixed = jnp.dot(weights.astype(jnp.bfloat16), v_ref[...], preferred_element_type=jnp.float32)
        acc_sc[...] = acc_sc[...] * factor + mixed
        m_sc[...] = new_best

    @pl.when(step == pl.num_programs(1) - 1)
    def _():
        o_ref[...] = (acc_sc[...] / l_sc[...]).astype(o_ref.dtype)


def flash_attention(queries, keys, values, query_start, token_first, first_block, count):
    tokens, heads, head_size = queries.shape
    q_rows = min(256, tokens)
    k_rows = 2 * q_rows
    blocks = tokens // q_rows
    steps = (W + q_rows) // k_rows + 1
    stacked = queries.reshape(blocks, q_rows, heads, head_size).transpose(0, 2, 1, 3)
    stacked = stacked.reshape(blocks * heads * q_rows, head_size)
    starts = jnp.broadcast_to(
        query_start.reshape(blocks, 1, q_rows), (blocks, heads, q_rows)
    ).reshape(blocks * heads * q_rows, 1)
    lowest = jnp.min(query_start.reshape(blocks, q_rows), axis=1)
    rows = heads * q_rows

    def kv_map(i, j, first, low):
        return ((i + first_block) * q_rows // k_rows + j, 0)

    out = pl.pallas_call(
        functools.partial(flash_kernel, q_rows, tokens, first_block),
        grid_spec=pltpu.PrefetchScalarGridSpec(
            num_scalar_prefetch=2,
            grid=(count, steps),
            in_specs=[
                pl.BlockSpec((rows, head_size), lambda i, j, first, low: (i + first_block, 0)),
                pl.BlockSpec((k_rows, head_size), kv_map),
                pl.BlockSpec((k_rows, head_size), kv_map),
                pl.BlockSpec((rows, 1), lambda i, j, first, low: (i + first_block, 0)),
            ],
            out_specs=pl.BlockSpec((rows, head_size), lambda i, j, first, low: (i, 0)),
            scratch_shapes=[
                pltpu.VMEM((rows, 1), jnp.float32),
                pltpu.VMEM((rows, 1), jnp.float32),
                pltpu.VMEM((rows, head_size), jnp.float32),
            ],
        ),
        out_shape=jax.ShapeDtypeStruct((count * rows, head_size), jnp.bfloat16),
        compiler_params=pltpu.CompilerParams(dimension_semantics=("arbitrary", "arbitrary")),
    )(token_first.reshape(1), lowest, stacked, keys, values, starts)
    return (
        out.reshape(count, heads, q_rows, head_size)
        .transpose(0, 2, 1, 3)
        .reshape(count * q_rows, heads * head_size)
    )


def body(tokens_in, norm_gain, q_weight, kv_weight, out_weight, segment_ids, page_table):
    seq_count = lax.axis_size("seq")
    mp_count = lax.axis_size("mp")
    seq_index = lax.axis_index("seq")
    mp_index = lax.axis_index("mp")
    tok_rows = tokens_in.shape[0]
    kv_heads = kv_weight.shape[0]
    head_size = kv_weight.shape[2] // 2
    ratio = mp_count // kv_heads
    own_head = mp_index // ratio
    kv_own = lax.dynamic_index_in_dim(kv_weight, own_head, 0, keepdims=False)
    q_columns = q_weight.shape[1]
    kv_columns = kv_own.shape[1]
    w_inputs = lax.all_gather(
        jnp.concatenate([kv_own, q_weight], axis=1), "seq", axis=0, tiled=True
    )
    w_output = lax.all_gather(out_weight, "seq", axis=0, tiled=True)
    inputs = tokens_in.astype(jnp.float32)
    meansq = jnp.mean(inputs * inputs, axis=-1, keepdims=True)
    normed = (inputs * lax.rsqrt(meansq + 1e-05) * norm_gain).astype(jnp.bfloat16)
    token_first = seq_index * tok_rows
    global_index = token_first + jnp.arange(tok_rows, dtype=jnp.int32)
    seg_values = jnp.arange(SEGS, dtype=jnp.int32)
    seg_hist = jnp.sum((segment_ids[:, None] == seg_values[None, :]).astype(jnp.int32), axis=0)
    seg_total = lax.psum(seg_hist, "seq")
    seg_first = jnp.cumsum(seg_total) - seg_total
    query_start = jnp.sum(
        jnp.where(segment_ids[:, None] == seg_values[None, :], seg_first[None, :], 0), axis=1
    )
    positions = global_index - query_start
    half = head_size // 2
    freqs = jnp.exp(jnp.arange(half, dtype=jnp.float32) * (-2.0 * math.log(10000.0) / head_size))
    angles = positions.astype(jnp.float32)[:, None] * freqs[None, :]
    cosine, sine_table = lax.optimization_barrier((jnp.cos(angles), jnp.sin(angles)))
    local_heads = q_columns // head_size
    projected = jnp.dot(normed, w_inputs[:, :kv_columns], preferred_element_type=jnp.float32)
    key_rows = rotate_half(projected[:, :head_size], cosine, sine_table).astype(jnp.bfloat16)
    value_rows = projected[:, head_size:].astype(jnp.bfloat16)
    keyval = jnp.concatenate([key_rows, value_rows], axis=1)
    earlier = from_behind(keyval, "seq", 1)
    queries = jnp.dot(normed, w_inputs[:, kv_columns:], preferred_element_type=jnp.float32)
    queries = queries.reshape(tok_rows, local_heads, head_size)
    queries = rotate_half(queries, cosine[:, None, :], sine_table[:, None, :]).astype(jnp.bfloat16)
    window = jnp.concatenate([earlier, keyval], axis=0)
    halves = 2
    blocks_all = tok_rows // min(256, tok_rows)
    outputs = []
    for part in range(halves):
        attended = flash_attention(
            queries,
            window[:, :head_size],
            window[:, head_size:],
            query_start,
            token_first,
            part * blocks_all // halves,
            blocks_all // halves,
        )
        partial_term = lax.dot_general(
            attended, w_output, (((1,), (1,)), ((), ())), preferred_element_type=jnp.float32
        )
        outputs.append(
            lax.psum_scatter(partial_term.astype(jnp.bfloat16), "mp", scatter_dimension=1, tiled=True)
        )
    layer_out = jnp.concatenate(outputs, axis=0)
    pages_dev = tok_rows // PAGE
    share_width = 2 * head_size // ratio
    share_index = mp_index % ratio
    share = lax.dynamic_slice_in_dim(keyval, share_index * share_width, share_width, 1)
    page_blocks = share.reshape(pages_dev, PAGE, share_width).transpose(0, 2, 1)
    owners = page_table // pages_dev
    local_slot = page_table % pages_dev
    spread = min(seq_count, pages_dev)
    capacity = pages_dev // spread
    page_order = jnp.arange(pages_dev, dtype=jnp.int32)
    same_owner = (owners[:, None] == owners[None, :]) & (page_order[None, :] < page_order[:, None])
    ranking = jnp.sum(same_owner.astype(jnp.int32), axis=1)
    lanes_all = seq_count * capacity
    send_lane = ((owners - seq_index) % seq_count) * capacity + ranking
    select = jnp.arange(lanes_all, dtype=jnp.int32)[:, None] == send_lane[None, :]
    outgoing = jnp.einsum(
        "sp,pfk->sfk", select.astype(jnp.bfloat16), page_blocks, preferred_element_type=jnp.float32
    ).astype(jnp.bfloat16)
    labels = jnp.sum(jnp.where(select, (local_slot + 1)[None, :], 0), axis=1)
    label_rows = jnp.broadcast_to(labels.astype(jnp.bfloat16)[:, None, None], (lanes_all, 1, PAGE))
    payload = jnp.concatenate([outgoing, label_rows], axis=1)
    arrived = [payload[:capacity]]
    for offset in range(1, seq_count):
        lanes = slice(offset * capacity, (offset + 1) * capacity)
        arrived.append(shift_round(payload[lanes], "seq", offset))
    landed = jnp.concatenate(arrived, axis=0)
    incoming = landed[:, :share_width]
    tags = landed[:, share_width, 0].astype(jnp.int32)
    placement = (tags[None, :] == (page_order + 1)[:, None]).astype(jnp.bfloat16)
    kv_cache = jnp.einsum(
        "ps,sfk->pfk", placement, incoming, preferred_element_type=jnp.float32
    ).astype(jnp.bfloat16)
    return (layer_out, kv_cache)


def solution(mesh):
    placed = (
        P("seq", None),
        P(),
        P("seq", "mp"),
        P(None, "seq", None),
        P("seq", "mp"),
        P("seq"),
        P("seq"),
    )
    return jax.shard_map(
        body,
        mesh=mesh,
        in_specs=placed,
        out_specs=(P("seq", "mp"), P("seq", "mp", None)),
        check_vma=False,
    )
```

```python
import functools
import math

import jax
import jax.numpy as jnp
from jax import lax
from jax.experimental import pallas as pl
from jax.experimental.pallas import tpu as pltpu
from jax.sharding import PartitionSpec as P

W = 2048
PAGE = 128
SEGS = 32


def from_behind(x, axis, by):
    peers = lax.axis_size(axis)
    pairs = [(i, i + by) for i in range(peers) if 0 <= i + by < peers]
    return lax.ppermute(x, axis, pairs)


def shift_round(x, axis, by):
    peers = lax.axis_size(axis)
    return lax.ppermute(x, axis, [(i, (i + by) % peers) for i in range(peers)])


def rotate_half(values, cosine, sine_table):
    half = values.shape[-1] // 2
    first_half = values[..., :half]
    second = values[..., half:]
    return jnp.concatenate(
        [first_half * cosine - second * sine_table, second * cosine + first_half * sine_table],
        axis=-1,
    )


def flash_kernel(q_rows, tokens, first_block, first_ref, lowest_ref, q_ref, k_ref, v_ref, qs_ref, o_ref, m_sc, l_sc, acc_sc):
    block = pl.program_id(0) + first_block
    step = pl.program_id(1)
    rows = q_ref.shape[0]
    k_rows = k_ref.shape[0]
    head_size = q_ref.shape[1]

    @pl.when(step == 0)
    def _():
        m_sc[...] = jnp.full(m_sc.shape, -1e30, jnp.float32)
        l_sc[...] = jnp.zeros(l_sc.shape, jnp.float32)
        acc_sc[...] = jnp.zeros(acc_sc.shape, jnp.float32)

    token_first = first_ref[0]
    query_first = token_first + block * q_rows
    key_first = token_first - tokens + (block * q_rows // k_rows + step) * k_rows
    key_last = key_first + k_rows - 1
    live = (key_last >= lowest_ref[block]) & (key_first <= query_first + q_rows - 1)
    live = live & (query_first - key_last < W)

    @pl.when(live)
    def _():
        scores = lax.dot_general(
            q_ref[...], k_ref[...], (((1,), (1,)), ((), ())), preferred_element_type=jnp.float32
        )
        column = lax.broadcasted_iota(jnp.int32, (1, k_rows), 1)
        row_ahead = (query_first - key_first) + lax.broadcasted_iota(jnp.int32, (rows, 1), 0) % q_rows
        ahead = (row_ahead - column).astype(jnp.uint32)
        keep = (ahead < jnp.uint32(W)) & (column >= qs_ref[...] - key_first)
        masked = jnp.where(keep, scores, -jnp.inf)
        best = m_sc[...]
        new_best = jnp.maximum(best, jnp.max(masked, axis=1, keepdims=True))
        weights = jnp.exp(masked - new_best)
        factor = jnp.exp(best - new_best)
        l_sc[...] = l_sc[...] * factor + jnp.sum(weights, axis=1, keepdims=True)
        mixed = jnp.dot(weights.astype(jnp.bfloat16), v_ref[...], preferred_element_type=jnp.float32)
        acc_sc[...] = acc_sc[...] * factor + mixed
        m_sc[...] = new_best

    @pl.when(step == pl.num_programs(1) - 1)
    def _():
        o_ref[...] = (acc_sc[...] / l_sc[...]).astype(o_ref.dtype)


def flash_attention(queries, keys, values, query_start, token_first, first_block, count):
    tokens, heads, head_size = queries.shape
    q_rows = min(256, tokens)
    k_rows = 2 * q_rows
    blocks = tokens // q_rows
    steps = (W + q_rows) // k_rows + 1
    scaled = queries * jnp.asarray(1.0 / math.sqrt(head_size), queries.dtype)
    stacked = scaled.reshape(blocks, q_rows, heads, head_size).transpose(0, 2, 1, 3)
    stacked = stacked.reshape(blocks * heads * q_rows, head_size)
    starts = jnp.broadcast_to(
        query_start.reshape(blocks, 1, q_rows), (blocks, heads, q_rows)
    ).reshape(blocks * heads * q_rows, 1)
    lowest = jnp.min(query_start.reshape(blocks, q_rows), axis=1)
    rows = heads * q_rows

    def kv_map(i, j, first, low):
        return ((i + first_block) * q_rows // k_rows + j, 0)

    out = pl.pallas_call(
        functools.partial(flash_kernel, q_rows, tokens, first_block),
        grid_spec=pltpu.PrefetchScalarGridSpec(
            num_scalar_prefetch=2,
            grid=(count, steps),
            in_specs=[
                pl.BlockSpec((rows, head_size), lambda i, j, first, low: (i + first_block, 0)),
                pl.BlockSpec((k_rows, head_size), kv_map),
                pl.BlockSpec((k_rows, head_size), kv_map),
                pl.BlockSpec((rows, 1), lambda i, j, first, low: (i + first_block, 0)),
            ],
            out_specs=pl.BlockSpec((rows, head_size), lambda i, j, first, low: (i, 0)),
            scratch_shapes=[
                pltpu.VMEM((rows, 1), jnp.float32),
                pltpu.VMEM((rows, 1), jnp.float32),
                pltpu.VMEM((rows, head_size), jnp.float32),
            ],
        ),
        out_shape=jax.ShapeDtypeStruct((count * rows, head_size), jnp.bfloat16),
        compiler_params=pltpu.CompilerParams(dimension_semantics=("arbitrary", "arbitrary")),
    )(token_first.reshape(1), lowest, stacked, keys, values, starts)
    return (
        out.reshape(count, heads, q_rows, head_size)
        .transpose(0, 2, 1, 3)
        .reshape(count * q_rows, heads * head_size)
    )


def body(tokens_in, norm_gain, q_weight, kv_weight, out_weight, segment_ids, page_table):
    seq_count = lax.axis_size("seq")
    mp_count = lax.axis_size("mp")
    seq_index = lax.axis_index("seq")
    mp_index = lax.axis_index("mp")
    tok_rows = tokens_in.shape[0]
    kv_heads = kv_weight.shape[0]
    head_size = kv_weight.shape[2] // 2
    ratio = mp_count // kv_heads
    own_head = mp_index // ratio
    kv_own = lax.dynamic_index_in_dim(kv_weight, own_head, 0, keepdims=False)
    q_columns = q_weight.shape[1]
    kv_columns = kv_own.shape[1]
    w_inputs = lax.all_gather(
        jnp.concatenate([kv_own, q_weight], axis=1), "seq", axis=0, tiled=True
    )
    w_output = lax.all_gather(out_weight, "seq", axis=0, tiled=True)
    inputs = tokens_in.astype(jnp.float32)
    meansq = jnp.mean(inputs * inputs, axis=-1, keepdims=True)
    normed = (inputs * lax.rsqrt(meansq + 1e-05) * norm_gain).astype(jnp.bfloat16)
    token_first = seq_index * tok_rows
    global_index = token_first + jnp.arange(tok_rows, dtype=jnp.int32)
    seg_values = jnp.arange(SEGS, dtype=jnp.int32)
    seg_hist = jnp.sum((segment_ids[:, None] == seg_values[None, :]).astype(jnp.int32), axis=0)
    seg_total = lax.psum(seg_hist, "seq")
    seg_first = jnp.cumsum(seg_total) - seg_total
    query_start = jnp.sum(
        jnp.where(segment_ids[:, None] == seg_values[None, :], seg_first[None, :], 0), axis=1
    )
    positions = global_index - query_start
    half = head_size // 2
    freqs = jnp.exp(jnp.arange(half, dtype=jnp.float32) * (-2.0 * math.log(10000.0) / head_size))
    angles = positions.astype(jnp.float32)[:, None] * freqs[None, :]
    cosine, sine_table = lax.optimization_barrier((jnp.cos(angles), jnp.sin(angles)))
    local_heads = q_columns // head_size
    projected = jnp.dot(normed, w_inputs[:, :kv_columns], preferred_element_type=jnp.float32)
    key_rows = rotate_half(projected[:, :head_size], cosine, sine_table).astype(jnp.bfloat16)
    value_rows = projected[:, head_size:].astype(jnp.bfloat16)
    keyval = jnp.concatenate([key_rows, value_rows], axis=1)
    earlier = from_behind(keyval, "seq", 1)
    queries = jnp.dot(normed, w_inputs[:, kv_columns:], preferred_element_type=jnp.float32)
    queries = queries.reshape(tok_rows, local_heads, head_size)
    queries = rotate_half(queries, cosine[:, None, :], sine_table[:, None, :]).astype(jnp.bfloat16)
    window = jnp.concatenate([earlier, keyval], axis=0)
    halves = 2
    blocks_all = tok_rows // min(256, tok_rows)
    outputs = []
    for part in range(halves):
        attended = flash_attention(
            queries,
            window[:, :head_size],
            window[:, head_size:],
            query_start,
            token_first,
            part * blocks_all // halves,
            blocks_all // halves,
        )
        partial_term = lax.dot_general(
            attended, w_output, (((1,), (1,)), ((), ())), preferred_element_type=jnp.float32
        )
        outputs.append(
            lax.psum_scatter(partial_term.astype(jnp.bfloat16), "mp", scatter_dimension=1, tiled=True)
        )
    layer_out = jnp.concatenate(outputs, axis=0)
    pages_dev = tok_rows // PAGE
    share_width = 2 * head_size // ratio
    share_index = mp_index % ratio
    share = lax.dynamic_slice_in_dim(keyval, share_index * share_width, share_width, 1)
    page_blocks = share.reshape(pages_dev, PAGE, share_width).transpose(0, 2, 1)
    owners = page_table // pages_dev
    local_slot = page_table % pages_dev
    spread = min(seq_count, pages_dev)
    capacity = pages_dev // spread
    page_order = jnp.arange(pages_dev, dtype=jnp.int32)
    same_owner = (owners[:, None] == owners[None, :]) & (page_order[None, :] < page_order[:, None])
    ranking = jnp.sum(same_owner.astype(jnp.int32), axis=1)
    lanes_all = seq_count * capacity
    send_lane = ((owners - seq_index) % seq_count) * capacity + ranking
    select = jnp.arange(lanes_all, dtype=jnp.int32)[:, None] == send_lane[None, :]
    outgoing = jnp.einsum(
        "sp,pfk->sfk", select.astype(jnp.bfloat16), page_blocks, preferred_element_type=jnp.float32
    ).astype(jnp.bfloat16)
    labels = jnp.sum(jnp.where(select, (local_slot + 1)[None, :], 0), axis=1)
    label_rows = jnp.broadcast_to(labels.astype(jnp.bfloat16)[:, None, None], (lanes_all, 1, PAGE))
    payload = jnp.concatenate([outgoing, label_rows], axis=1)
    arrived = [payload[:capacity]]
    for offset in range(1, seq_count):
        lanes = slice(offset * capacity, (offset + 1) * capacity)
        arrived.append(shift_round(payload[lanes], "seq", offset))
    landed = jnp.concatenate(arrived, axis=0)
    incoming = landed[:, :share_width]
    tags = landed[:, share_width, 0].astype(jnp.int32)
    placement = (tags[None, :] == (page_order + 1)[:, None]).astype(jnp.bfloat16)
    kv_cache = jnp.einsum(
        "ps,sfk->pfk", placement, incoming, preferred_element_type=jnp.float32
    ).astype(jnp.bfloat16)
    return (layer_out, kv_cache)


def solution(mesh):
    placed = (
        P("seq", None),
        P(),
        P("seq", "mp"),
        P(None, "seq", None),
        P("seq", "mp"),
        P("seq"),
        P("seq"),
    )
    return jax.shard_map(
        body,
        mesh=mesh,
        in_specs=placed,
        out_specs=(P("seq", "mp"), P("seq", "mp", None)),
        check_vma=False,
    )
```

```python
import functools
import math

import jax
import jax.numpy as jnp
from jax import lax
from jax.experimental import pallas as pl
from jax.experimental.pallas import tpu as pltpu
from jax.sharding import PartitionSpec as P

W = 2048
PAGE = 128
SEGS = 32


def from_behind(x, axis, by):
    peers = lax.axis_size(axis)
    pairs = [(i, i + by) for i in range(peers) if 0 <= i + by < peers]
    return lax.ppermute(x, axis, pairs)


def shift_round(x, axis, by):
    peers = lax.axis_size(axis)
    return lax.ppermute(x, axis, [(i, (i + by) % peers) for i in range(peers)])


def rotate_half(values, cosine, sine_table):
    half = values.shape[-1] // 2
    first_half = values[..., :half]
    second = values[..., half:]
    return jnp.concatenate(
        [first_half * cosine - second * sine_table, second * cosine + first_half * sine_table],
        axis=-1,
    )


def flash_kernel(q_rows, tokens, first_block, first_ref, lowest_ref, q_ref, k_ref, v_ref, qs_ref, o_ref, m_sc, acc_sc):
    block = pl.program_id(0) + first_block
    step = pl.program_id(1)
    rows = q_ref.shape[0]
    k_rows = k_ref.shape[0]
    head_size = q_ref.shape[1]

    @pl.when(step == 0)
    def _():
        m_sc[...] = jnp.full(m_sc.shape, -1e30, jnp.float32)
        acc_sc[...] = jnp.zeros(acc_sc.shape, jnp.float32)

    token_first = first_ref[0]
    query_first = token_first + block * q_rows
    key_first = token_first - tokens + (block * q_rows // k_rows + step) * k_rows
    key_last = key_first + k_rows - 1
    live = (key_last >= lowest_ref[block]) & (key_first <= query_first + q_rows - 1)
    live = live & (query_first - key_last < W)

    @pl.when(live)
    def _():
        scores = lax.dot_general(
            q_ref[...], k_ref[...], (((1,), (1,)), ((), ())), preferred_element_type=jnp.float32
        )
        column = lax.broadcasted_iota(jnp.int32, (1, k_rows), 1)
        row_ahead = (query_first - key_first) + lax.broadcasted_iota(jnp.int32, (rows, 1), 0) % q_rows
        ahead = (row_ahead - column).astype(jnp.uint32)
        keep = (ahead < jnp.uint32(W)) & (column >= qs_ref[...] - key_first)
        masked = jnp.where(keep, scores, -jnp.inf)
        best = m_sc[...]
        new_best = jnp.maximum(best, jnp.max(masked, axis=1, keepdims=True))
        weights = jnp.exp(masked - new_best)
        factor = jnp.exp(best - new_best)
        mixed = jnp.dot(weights.astype(jnp.bfloat16), v_ref[...], preferred_element_type=jnp.float32)
        acc_sc[...] = acc_sc[...] * factor + mixed
        m_sc[...] = new_best

    @pl.when(step == pl.num_programs(1) - 1)
    def _():
        head_size = o_ref.shape[1]
        totals = acc_sc[:, head_size:head_size + 1]
        o_ref[...] = (acc_sc[:, :head_size] / totals).astype(o_ref.dtype)


def flash_attention(queries, keys, values, query_start, token_first, first_block, count):
    tokens, heads, head_size = queries.shape
    q_rows = min(256, tokens)
    k_rows = 2 * q_rows
    blocks = tokens // q_rows
    steps = (W + q_rows) // k_rows + 1
    scaled = queries * jnp.asarray(1.0 / math.sqrt(head_size), queries.dtype)
    stacked = scaled.reshape(blocks, q_rows, heads, head_size).transpose(0, 2, 1, 3)
    stacked = stacked.reshape(blocks * heads * q_rows, head_size)
    starts = jnp.broadcast_to(
        query_start.reshape(blocks, 1, q_rows), (blocks, heads, q_rows)
    ).reshape(blocks * heads * q_rows, 1)
    lowest = jnp.min(query_start.reshape(blocks, q_rows), axis=1)
    rows = heads * q_rows
    counted = jnp.zeros((values.shape[0], head_size), values.dtype).at[:, 0].set(1)
    values = jnp.concatenate([values, counted], axis=1)

    def kv_map(i, j, first, low):
        return ((i + first_block) * q_rows // k_rows + j, 0)

    out = pl.pallas_call(
        functools.partial(flash_kernel, q_rows, tokens, first_block),
        grid_spec=pltpu.PrefetchScalarGridSpec(
            num_scalar_prefetch=2,
            grid=(count, steps),
            in_specs=[
                pl.BlockSpec((rows, head_size), lambda i, j, first, low: (i + first_block, 0)),
                pl.BlockSpec((k_rows, head_size), kv_map),
                pl.BlockSpec((k_rows, 2 * head_size), kv_map),
                pl.BlockSpec((rows, 1), lambda i, j, first, low: (i + first_block, 0)),
            ],
            out_specs=pl.BlockSpec((rows, head_size), lambda i, j, first, low: (i, 0)),
            scratch_shapes=[
                pltpu.VMEM((rows, 1), jnp.float32),
                pltpu.VMEM((rows, 2 * head_size), jnp.float32),
            ],
        ),
        out_shape=jax.ShapeDtypeStruct((count * rows, head_size), jnp.bfloat16),
        compiler_params=pltpu.CompilerParams(dimension_semantics=("arbitrary", "arbitrary")),
    )(token_first.reshape(1), lowest, stacked, keys, values, starts)
    return (
        out.reshape(count, heads, q_rows, head_size)
        .transpose(0, 2, 1, 3)
        .reshape(count * q_rows, heads * head_size)
    )


def body(tokens_in, norm_gain, q_weight, kv_weight, out_weight, segment_ids, page_table):
    seq_count = lax.axis_size("seq")
    mp_count = lax.axis_size("mp")
    seq_index = lax.axis_index("seq")
    mp_index = lax.axis_index("mp")
    tok_rows = tokens_in.shape[0]
    kv_heads = kv_weight.shape[0]
    head_size = kv_weight.shape[2] // 2
    ratio = mp_count // kv_heads
    own_head = mp_index // ratio
    kv_own = lax.dynamic_index_in_dim(kv_weight, own_head, 0, keepdims=False)
    q_columns = q_weight.shape[1]
    kv_columns = kv_own.shape[1]
    w_inputs = lax.all_gather(
        jnp.concatenate([kv_own, q_weight], axis=1), "seq", axis=0, tiled=True
    )
    w_output = lax.all_gather(out_weight, "seq", axis=0, tiled=True)
    inputs = tokens_in.astype(jnp.float32)
    meansq = jnp.mean(inputs * inputs, axis=-1, keepdims=True)
    normed = (inputs * lax.rsqrt(meansq + 1e-05) * norm_gain).astype(jnp.bfloat16)
    token_first = seq_index * tok_rows
    global_index = token_first + jnp.arange(tok_rows, dtype=jnp.int32)
    seg_values = jnp.arange(SEGS, dtype=jnp.int32)
    seg_hist = jnp.sum((segment_ids[:, None] == seg_values[None, :]).astype(jnp.int32), axis=0)
    seg_total = lax.psum(seg_hist, "seq")
    seg_first = jnp.cumsum(seg_total) - seg_total
    query_start = jnp.sum(
        jnp.where(segment_ids[:, None] == seg_values[None, :], seg_first[None, :], 0), axis=1
    )
    positions = global_index - query_start
    half = head_size // 2
    freqs = jnp.exp(jnp.arange(half, dtype=jnp.float32) * (-2.0 * math.log(10000.0) / head_size))
    angles = positions.astype(jnp.float32)[:, None] * freqs[None, :]
    cosine, sine_table = lax.optimization_barrier((jnp.cos(angles), jnp.sin(angles)))
    local_heads = q_columns // head_size
    projected = jnp.dot(normed, w_inputs[:, :kv_columns], preferred_element_type=jnp.float32)
    key_rows = rotate_half(projected[:, :head_size], cosine, sine_table).astype(jnp.bfloat16)
    value_rows = projected[:, head_size:].astype(jnp.bfloat16)
    keyval = jnp.concatenate([key_rows, value_rows], axis=1)
    earlier = from_behind(keyval, "seq", 1)
    queries = jnp.dot(normed, w_inputs[:, kv_columns:], preferred_element_type=jnp.float32)
    queries = queries.reshape(tok_rows, local_heads, head_size)
    queries = rotate_half(queries, cosine[:, None, :], sine_table[:, None, :]).astype(jnp.bfloat16)
    window = jnp.concatenate([earlier, keyval], axis=0)
    halves = 2
    blocks_all = tok_rows // min(256, tok_rows)
    outputs = []
    for part in range(halves):
        attended = flash_attention(
            queries,
            window[:, :head_size],
            window[:, head_size:],
            query_start,
            token_first,
            part * blocks_all // halves,
            blocks_all // halves,
        )
        partial_term = lax.dot_general(
            attended, w_output, (((1,), (1,)), ((), ())), preferred_element_type=jnp.float32
        )
        outputs.append(
            lax.psum_scatter(partial_term.astype(jnp.bfloat16), "mp", scatter_dimension=1, tiled=True)
        )
    layer_out = jnp.concatenate(outputs, axis=0)
    pages_dev = tok_rows // PAGE
    share_width = 2 * head_size // ratio
    share_index = mp_index % ratio
    share = lax.dynamic_slice_in_dim(keyval, share_index * share_width, share_width, 1)
    page_blocks = share.reshape(pages_dev, PAGE, share_width).transpose(0, 2, 1)
    owners = page_table // pages_dev
    local_slot = page_table % pages_dev
    spread = min(seq_count, pages_dev)
    capacity = pages_dev // spread
    page_order = jnp.arange(pages_dev, dtype=jnp.int32)
    same_owner = (owners[:, None] == owners[None, :]) & (page_order[None, :] < page_order[:, None])
    ranking = jnp.sum(same_owner.astype(jnp.int32), axis=1)
    lanes_all = seq_count * capacity
    send_lane = ((owners - seq_index) % seq_count) * capacity + ranking
    select = jnp.arange(lanes_all, dtype=jnp.int32)[:, None] == send_lane[None, :]
    outgoing = jnp.einsum(
        "sp,pfk->sfk", select.astype(jnp.bfloat16), page_blocks, preferred_element_type=jnp.float32
    ).astype(jnp.bfloat16)
    labels = jnp.sum(jnp.where(select, (local_slot + 1)[None, :], 0), axis=1)
    label_rows = jnp.broadcast_to(labels.astype(jnp.bfloat16)[:, None, None], (lanes_all, 1, PAGE))
    payload = jnp.concatenate([outgoing, label_rows], axis=1)
    arrived = [payload[:capacity]]
    for offset in range(1, seq_count):
        lanes = slice(offset * capacity, (offset + 1) * capacity)
        arrived.append(shift_round(payload[lanes], "seq", offset))
    landed = jnp.concatenate(arrived, axis=0)
    incoming = landed[:, :share_width]
    tags = landed[:, share_width, 0].astype(jnp.int32)
    placement = (tags[None, :] == (page_order + 1)[:, None]).astype(jnp.bfloat16)
    kv_cache = jnp.einsum(
        "ps,sfk->pfk", placement, incoming, preferred_element_type=jnp.float32
    ).astype(jnp.bfloat16)
    return (layer_out, kv_cache)


def solution(mesh):
    placed = (
        P("seq", None),
        P(),
        P("seq", "mp"),
        P(None, "seq", None),
        P("seq", "mp"),
        P("seq"),
        P("seq"),
    )
    return jax.shard_map(
        body,
        mesh=mesh,
        in_specs=placed,
        out_specs=(P("seq", "mp"), P("seq", "mp", None)),
        check_vma=False,
    )
```

```python
import functools
import math

import jax
import jax.numpy as jnp
from jax import lax
from jax.experimental import pallas as pl
from jax.experimental.pallas import tpu as pltpu
from jax.sharding import PartitionSpec as P

W = 2048
PAGE = 128
SEGS = 32


def from_behind(x, axis, by):
    peers = lax.axis_size(axis)
    pairs = [(i, i + by) for i in range(peers) if 0 <= i + by < peers]
    return lax.ppermute(x, axis, pairs)


def shift_round(x, axis, by):
    peers = lax.axis_size(axis)
    return lax.ppermute(x, axis, [(i, (i + by) % peers) for i in range(peers)])


def rotate_half(values, cosine, sine_table):
    half = values.shape[-1] // 2
    first_half = values[..., :half]
    second = values[..., half:]
    return jnp.concatenate(
        [first_half * cosine - second * sine_table, second * cosine + first_half * sine_table],
        axis=-1,
    )


def flash_kernel(q_rows, tokens, first_block, first_ref, lowest_ref, q_ref, k_ref, v_ref, qs_ref, o_ref, m_sc, acc_sc):
    block = pl.program_id(0) + first_block
    step = pl.program_id(1)
    rows = q_ref.shape[0]
    k_rows = k_ref.shape[0]
    head_size = q_ref.shape[1]

    @pl.when(step == 0)
    def _():
        m_sc[...] = jnp.full(m_sc.shape, -1e30, jnp.float32)
        acc_sc[...] = jnp.zeros(acc_sc.shape, jnp.float32)

    token_first = first_ref[0]
    query_first = token_first + block * q_rows
    key_first = token_first - tokens + (block * q_rows // k_rows + step) * k_rows
    key_last = key_first + k_rows - 1
    live = (key_last >= lowest_ref[block]) & (key_first <= query_first + q_rows - 1)
    live = live & (query_first - key_last < W)

    @pl.when(live)
    def _():
        scores = lax.dot_general(
            q_ref[...], k_ref[...], (((1,), (1,)), ((), ())), preferred_element_type=jnp.float32
        )
        column = lax.broadcasted_iota(jnp.int32, (1, k_rows), 1)
        row_ahead = (query_first - key_first) + lax.broadcasted_iota(jnp.int32, (rows, 1), 0) % q_rows
        ahead = (row_ahead - column).astype(jnp.uint32)
        keep = (ahead < jnp.uint32(W)) & (column >= qs_ref[...] - key_first)
        masked = jnp.where(keep, scores, -jnp.inf)
        best = m_sc[...]
        new_best = jnp.maximum(best, jnp.max(masked, axis=1, keepdims=True))
        weights = jnp.exp(masked - new_best)
        factor = jnp.exp(best - new_best)
        mixed = jnp.dot(weights.astype(jnp.bfloat16), v_ref[...], preferred_element_type=jnp.float32)
        acc_sc[...] = acc_sc[...] * factor + mixed
        m_sc[...] = new_best

    @pl.when(step == pl.num_programs(1) - 1)
    def _():
        head_size = o_ref.shape[1]
        totals = acc_sc[:, head_size:head_size + 1]
        o_ref[...] = (acc_sc[:, :head_size] / totals).astype(o_ref.dtype)


def flash_attention(queries, keys, values, query_start, token_first, first_block, count):
    tokens, heads, head_size = queries.shape
    q_rows = min(256, tokens)
    k_rows = 2 * q_rows
    blocks = tokens // q_rows
    steps = (W + q_rows) // k_rows + 1
    scaled = queries * jnp.asarray(1.0 / math.sqrt(head_size), queries.dtype)
    stacked = scaled.reshape(blocks, q_rows, heads, head_size).transpose(0, 2, 1, 3)
    stacked = stacked.reshape(blocks * heads * q_rows, head_size)
    starts = jnp.broadcast_to(
        query_start.reshape(blocks, 1, q_rows), (blocks, heads, q_rows)
    ).reshape(blocks * heads * q_rows, 1)
    lowest = jnp.min(query_start.reshape(blocks, q_rows), axis=1)
    rows = heads * q_rows
    counted = jnp.zeros((values.shape[0], head_size), values.dtype).at[:, 0].set(1)
    values = jnp.concatenate([values, counted], axis=1)

    def kv_map(i, j, first, low):
        return ((i + first_block) * q_rows // k_rows + j, 0)

    out = pl.pallas_call(
        functools.partial(flash_kernel, q_rows, tokens, first_block),
        grid_spec=pltpu.PrefetchScalarGridSpec(
            num_scalar_prefetch=2,
            grid=(count, steps),
            in_specs=[
                pl.BlockSpec((rows, head_size), lambda i, j, first, low: (i + first_block, 0)),
                pl.BlockSpec((k_rows, head_size), kv_map),
                pl.BlockSpec((k_rows, 2 * head_size), kv_map),
                pl.BlockSpec((rows, 1), lambda i, j, first, low: (i + first_block, 0)),
            ],
            out_specs=pl.BlockSpec((rows, head_size), lambda i, j, first, low: (i, 0)),
            scratch_shapes=[
                pltpu.VMEM((rows, 1), jnp.float32),
                pltpu.VMEM((rows, 2 * head_size), jnp.float32),
            ],
        ),
        out_shape=jax.ShapeDtypeStruct((count * rows, head_size), jnp.bfloat16),
        compiler_params=pltpu.CompilerParams(dimension_semantics=("arbitrary", "arbitrary")),
    )(token_first.reshape(1), lowest, stacked, keys, values, starts)
    return (
        out.reshape(count, heads, q_rows, head_size)
        .transpose(0, 2, 1, 3)
        .reshape(count * q_rows, heads * head_size)
    )


def body(tokens_in, norm_gain, q_weight, kv_weight, out_weight, segment_ids, page_table):
    seq_count = lax.axis_size("seq")
    mp_count = lax.axis_size("mp")
    seq_index = lax.axis_index("seq")
    mp_index = lax.axis_index("mp")
    tok_rows = tokens_in.shape[0]
    kv_heads = kv_weight.shape[0]
    head_size = kv_weight.shape[2] // 2
    ratio = mp_count // kv_heads
    own_head = mp_index // ratio
    kv_own = lax.dynamic_index_in_dim(kv_weight, own_head, 0, keepdims=False)
    q_columns = q_weight.shape[1]
    kv_columns = kv_own.shape[1]
    w_inputs = lax.all_gather(
        jnp.concatenate([kv_own, q_weight], axis=1), "seq", axis=0, tiled=True
    )
    w_output = lax.all_gather(out_weight, "seq", axis=0, tiled=True)
    inputs = tokens_in.astype(jnp.float32)
    meansq = jnp.mean(inputs * inputs, axis=-1, keepdims=True)
    normed = (inputs * lax.rsqrt(meansq + 1e-05) * norm_gain).astype(jnp.bfloat16)
    token_first = seq_index * tok_rows
    global_index = token_first + jnp.arange(tok_rows, dtype=jnp.int32)
    seg_values = jnp.arange(SEGS, dtype=jnp.int32)
    seg_hist = jnp.sum((segment_ids[:, None] == seg_values[None, :]).astype(jnp.int32), axis=0)
    seg_total = lax.psum(seg_hist, "seq")
    seg_first = jnp.cumsum(seg_total) - seg_total
    query_start = jnp.sum(
        jnp.where(segment_ids[:, None] == seg_values[None, :], seg_first[None, :], 0), axis=1
    )
    positions = global_index - query_start
    half = head_size // 2
    freqs = jnp.exp(jnp.arange(half, dtype=jnp.float32) * (-2.0 * math.log(10000.0) / head_size))
    angles = positions.astype(jnp.float32)[:, None] * freqs[None, :]
    cosine, sine_table = lax.optimization_barrier((jnp.cos(angles), jnp.sin(angles)))
    local_heads = q_columns // head_size
    projected = jnp.dot(normed, w_inputs[:, :kv_columns], preferred_element_type=jnp.float32)
    key_rows = rotate_half(projected[:, :head_size], cosine, sine_table).astype(jnp.bfloat16)
    value_rows = projected[:, head_size:].astype(jnp.bfloat16)
    keyval = jnp.concatenate([key_rows, value_rows], axis=1)
    earlier = from_behind(keyval, "seq", 1)
    queries = jnp.dot(normed, w_inputs[:, kv_columns:], preferred_element_type=jnp.float32)
    queries = queries.reshape(tok_rows, local_heads, head_size)
    queries = rotate_half(queries, cosine[:, None, :], sine_table[:, None, :]).astype(jnp.bfloat16)
    window = jnp.concatenate([earlier, keyval], axis=0)
    pages_dev = tok_rows // PAGE
    share_width = 2 * head_size // ratio
    share_index = mp_index % ratio
    share = lax.dynamic_slice_in_dim(keyval, share_index * share_width, share_width, 1)
    page_blocks = share.reshape(pages_dev, PAGE, share_width).transpose(0, 2, 1)
    owners = page_table // pages_dev
    local_slot = page_table % pages_dev
    spread = min(seq_count, pages_dev)
    capacity = pages_dev // spread
    page_order = jnp.arange(pages_dev, dtype=jnp.int32)
    same_owner = (owners[:, None] == owners[None, :]) & (page_order[None, :] < page_order[:, None])
    ranking = jnp.sum(same_owner.astype(jnp.int32), axis=1)
    lanes_all = seq_count * capacity
    send_lane = ((owners - seq_index) % seq_count) * capacity + ranking
    select = jnp.arange(lanes_all, dtype=jnp.int32)[:, None] == send_lane[None, :]
    outgoing = jnp.einsum(
        "sp,pfk->sfk", select.astype(jnp.bfloat16), page_blocks, preferred_element_type=jnp.float32
    ).astype(jnp.bfloat16)
    labels = jnp.sum(jnp.where(select, (local_slot + 1)[None, :], 0), axis=1)
    label_rows = jnp.broadcast_to(labels.astype(jnp.bfloat16)[:, None, None], (lanes_all, 1, PAGE))
    payload = jnp.concatenate([outgoing, label_rows], axis=1)
    arrived = [payload[:capacity]]
    for offset in range(1, seq_count):
        lanes = slice(offset * capacity, (offset + 1) * capacity)
        arrived.append(shift_round(payload[lanes], "seq", offset))
    landed = jnp.concatenate(arrived, axis=0)
    incoming = landed[:, :share_width]
    tags = landed[:, share_width, 0].astype(jnp.int32)
    halves = 2
    blocks_all = tok_rows // min(256, tok_rows)
    outputs = []
    for part in range(halves):
        if part == 1:
            queries, landed = lax.optimization_barrier((queries, landed))
        attended = flash_attention(
            queries,
            window[:, :head_size],
            window[:, head_size:],
            query_start,
            token_first,
            part * blocks_all // halves,
            blocks_all // halves,
        )
        partial_term = lax.dot_general(
            attended, w_output, (((1,), (1,)), ((), ())), preferred_element_type=jnp.float32
        )
        outputs.append(
            lax.psum_scatter(partial_term.astype(jnp.bfloat16), "mp", scatter_dimension=1, tiled=True)
        )
    layer_out = jnp.concatenate(outputs, axis=0)
    placement = (tags[None, :] == (page_order + 1)[:, None]).astype(jnp.bfloat16)
    kv_cache = jnp.einsum(
        "ps,sfk->pfk", placement, incoming, preferred_element_type=jnp.float32
    ).astype(jnp.bfloat16)
    return (layer_out, kv_cache)


def solution(mesh):
    placed = (
        P("seq", None),
        P(),
        P("seq", "mp"),
        P(None, "seq", None),
        P("seq", "mp"),
        P("seq"),
        P("seq"),
    )
    return jax.shard_map(
        body,
        mesh=mesh,
        in_specs=placed,
        out_specs=(P("seq", "mp"), P("seq", "mp", None)),
        check_vma=False,
    )
```

```python
import functools
import math

import jax
import jax.numpy as jnp
from jax import lax
from jax.experimental import pallas as pl
from jax.experimental.pallas import tpu as pltpu
from jax.sharding import PartitionSpec as P

W = 2048
PAGE = 128
SEGS = 32


def from_behind(x, axis, by):
    peers = lax.axis_size(axis)
    pairs = [(i, i + by) for i in range(peers) if 0 <= i + by < peers]
    return lax.ppermute(x, axis, pairs)


def shift_round(x, axis, by):
    peers = lax.axis_size(axis)
    return lax.ppermute(x, axis, [(i, (i + by) % peers) for i in range(peers)])


def rotate_half(values, cosine, sine_table):
    half = values.shape[-1] // 2
    first_half = values[..., :half]
    second = values[..., half:]
    return jnp.concatenate(
        [first_half * cosine - second * sine_table, second * cosine + first_half * sine_table],
        axis=-1,
    )


def flash_kernel(q_rows, tokens, first_block, first_ref, lowest_ref, q_ref, k_ref, v_ref, qs_ref, o_ref, m_sc, acc_sc):
    block = pl.program_id(0) + first_block
    step = pl.program_id(1)
    rows = q_ref.shape[0]
    k_rows = k_ref.shape[0]
    head_size = q_ref.shape[1]

    @pl.when(step == 0)
    def _():
        m_sc[...] = jnp.full(m_sc.shape, -1e30, jnp.float32)
        acc_sc[...] = jnp.zeros(acc_sc.shape, jnp.float32)

    token_first = first_ref[0]
    query_first = token_first + block * q_rows
    key_first = token_first - tokens + (block * q_rows // k_rows + step) * k_rows
    key_last = key_first + k_rows - 1
    live = (key_last >= lowest_ref[block]) & (key_first <= query_first + q_rows - 1)
    live = live & (query_first - key_last < W)

    @pl.when(live)
    def _():
        scores = lax.dot_general(
            q_ref[...], k_ref[...], (((1,), (1,)), ((), ())), preferred_element_type=jnp.float32
        )
        column = lax.broadcasted_iota(jnp.int32, (1, k_rows), 1)
        row_ahead = (query_first - key_first) + lax.broadcasted_iota(jnp.int32, (rows, 1), 0) % q_rows
        ahead = (row_ahead - column).astype(jnp.uint32)
        keep = (ahead < jnp.uint32(W)) & (column >= qs_ref[...] - key_first)
        masked = jnp.where(keep, scores, -jnp.inf)
        best = m_sc[...]
        new_best = jnp.maximum(best, jnp.max(masked, axis=1, keepdims=True))
        weights = jnp.exp(masked - new_best)
        factor = jnp.exp(best - new_best)
        mixed = jnp.dot(weights.astype(jnp.bfloat16), v_ref[...], preferred_element_type=jnp.float32)
        acc_sc[...] = acc_sc[...] * factor + mixed
        m_sc[...] = new_best

    @pl.when(step == pl.num_programs(1) - 1)
    def _():
        head_size = o_ref.shape[1]
        totals = acc_sc[:, head_size:head_size + 1]
        o_ref[...] = (acc_sc[:, :head_size] / totals).astype(o_ref.dtype)


def flash_attention(queries, keys, values, query_start, token_first, first_block, count):
    tokens, heads, head_size = queries.shape
    q_rows = min(256, tokens)
    k_rows = 2 * q_rows
    blocks = tokens // q_rows
    steps = (W + q_rows) // k_rows + 1
    scaled = queries * jnp.asarray(1.0 / math.sqrt(head_size), queries.dtype)
    stacked = scaled.reshape(blocks, q_rows, heads, head_size).transpose(0, 2, 1, 3)
    stacked = stacked.reshape(blocks * heads * q_rows, head_size)
    starts = jnp.broadcast_to(
        query_start.reshape(blocks, 1, q_rows), (blocks, heads, q_rows)
    ).reshape(blocks * heads * q_rows, 1)
    lowest = jnp.min(query_start.reshape(blocks, q_rows), axis=1)
    rows = heads * q_rows
    counted = jnp.zeros((values.shape[0], head_size), values.dtype).at[:, 0].set(1)
    values = jnp.concatenate([values, counted], axis=1)

    def kv_map(i, j, first, low):
        return ((i + first_block) * q_rows // k_rows + j, 0)

    out = pl.pallas_call(
        functools.partial(flash_kernel, q_rows, tokens, first_block),
        grid_spec=pltpu.PrefetchScalarGridSpec(
            num_scalar_prefetch=2,
            grid=(count, steps),
            in_specs=[
                pl.BlockSpec((rows, head_size), lambda i, j, first, low: (i + first_block, 0)),
                pl.BlockSpec((k_rows, head_size), kv_map),
                pl.BlockSpec((k_rows, 2 * head_size), kv_map),
                pl.BlockSpec((rows, 1), lambda i, j, first, low: (i + first_block, 0)),
            ],
            out_specs=pl.BlockSpec((rows, head_size), lambda i, j, first, low: (i, 0)),
            scratch_shapes=[
                pltpu.VMEM((rows, 1), jnp.float32),
                pltpu.VMEM((rows, 2 * head_size), jnp.float32),
            ],
        ),
        out_shape=jax.ShapeDtypeStruct((count * rows, head_size), jnp.bfloat16),
        compiler_params=pltpu.CompilerParams(dimension_semantics=("arbitrary", "arbitrary")),
    )(token_first.reshape(1), lowest, stacked, keys, values, starts)
    return (
        out.reshape(count, heads, q_rows, head_size)
        .transpose(0, 2, 1, 3)
        .reshape(count * q_rows, heads * head_size)
    )


def body(tokens_in, norm_gain, q_weight, kv_weight, out_weight, segment_ids, page_table):
    seq_count = lax.axis_size("seq")
    mp_count = lax.axis_size("mp")
    seq_index = lax.axis_index("seq")
    mp_index = lax.axis_index("mp")
    tok_rows = tokens_in.shape[0]
    kv_heads = kv_weight.shape[0]
    head_size = kv_weight.shape[2] // 2
    ratio = mp_count // kv_heads
    own_head = mp_index // ratio
    kv_own = lax.dynamic_index_in_dim(kv_weight, own_head, 0, keepdims=False)
    q_columns = q_weight.shape[1]
    kv_columns = kv_own.shape[1]
    w_inputs = lax.all_gather(
        jnp.concatenate([kv_own, q_weight], axis=1), "seq", axis=0, tiled=True
    )
    w_output = lax.all_gather(out_weight, "seq", axis=0, tiled=True)
    inputs = tokens_in.astype(jnp.float32)
    meansq = jnp.mean(inputs * inputs, axis=-1, keepdims=True)
    normed = (inputs * lax.rsqrt(meansq + 1e-05) * norm_gain).astype(jnp.bfloat16)
    token_first = seq_index * tok_rows
    global_index = token_first + jnp.arange(tok_rows, dtype=jnp.int32)
    seg_values = jnp.arange(SEGS, dtype=jnp.int32)
    seg_hist = jnp.sum((segment_ids[:, None] == seg_values[None, :]).astype(jnp.int32), axis=0)
    seg_total = lax.psum(seg_hist, "seq")
    seg_first = jnp.cumsum(seg_total) - seg_total
    query_start = jnp.sum(
        jnp.where(segment_ids[:, None] == seg_values[None, :], seg_first[None, :], 0), axis=1
    )
    positions = global_index - query_start
    half = head_size // 2
    freqs = jnp.exp(jnp.arange(half, dtype=jnp.float32) * (-2.0 * math.log(10000.0) / head_size))
    angles = positions.astype(jnp.float32)[:, None] * freqs[None, :]
    cosine, sine_table = lax.optimization_barrier((jnp.cos(angles), jnp.sin(angles)))
    local_heads = q_columns // head_size
    projected = jnp.dot(normed, w_inputs[:, :kv_columns], preferred_element_type=jnp.float32)
    key_rows = rotate_half(projected[:, :head_size], cosine, sine_table).astype(jnp.bfloat16)
    value_rows = projected[:, head_size:].astype(jnp.bfloat16)
    keyval = jnp.concatenate([key_rows, value_rows], axis=1)
    earlier = from_behind(keyval, "seq", 1)
    queries = jnp.dot(normed, w_inputs[:, kv_columns:], preferred_element_type=jnp.float32)
    queries = queries.reshape(tok_rows, local_heads, head_size)
    queries = rotate_half(queries, cosine[:, None, :], sine_table[:, None, :]).astype(jnp.bfloat16)
    window = jnp.concatenate([earlier, keyval], axis=0)
    blocks_all = tok_rows // min(256, tok_rows)
    outputs = []
    split_at = (3 * blocks_all) // 8
    for first, count in ((0, split_at), (split_at, blocks_all - split_at)):
        attended = flash_attention(
            queries,
            window[:, :head_size],
            window[:, head_size:],
            query_start,
            token_first,
            first,
            count,
        )
        partial_term = lax.dot_general(
            attended, w_output, (((1,), (1,)), ((), ())), preferred_element_type=jnp.float32
        )
        outputs.append(
            lax.psum_scatter(partial_term.astype(jnp.bfloat16), "mp", scatter_dimension=1, tiled=True)
        )
    layer_out = jnp.concatenate(outputs, axis=0)
    pages_dev = tok_rows // PAGE
    share_width = 2 * head_size // ratio
    share_index = mp_index % ratio
    share = lax.dynamic_slice_in_dim(keyval, share_index * share_width, share_width, 1)
    page_blocks = share.reshape(pages_dev, PAGE, share_width).transpose(0, 2, 1)
    owners = page_table // pages_dev
    local_slot = page_table % pages_dev
    spread = min(seq_count, pages_dev)
    capacity = pages_dev // spread
    page_order = jnp.arange(pages_dev, dtype=jnp.int32)
    same_owner = (owners[:, None] == owners[None, :]) & (page_order[None, :] < page_order[:, None])
    ranking = jnp.sum(same_owner.astype(jnp.int32), axis=1)
    lanes_all = seq_count * capacity
    send_lane = ((owners - seq_index) % seq_count) * capacity + ranking
    select = jnp.arange(lanes_all, dtype=jnp.int32)[:, None] == send_lane[None, :]
    outgoing = jnp.einsum(
        "sp,pfk->sfk", select.astype(jnp.bfloat16), page_blocks, preferred_element_type=jnp.float32
    ).astype(jnp.bfloat16)
    labels = jnp.sum(jnp.where(select, (local_slot + 1)[None, :], 0), axis=1)
    label_rows = jnp.broadcast_to(labels.astype(jnp.bfloat16)[:, None, None], (lanes_all, 1, PAGE))
    payload = jnp.concatenate([outgoing, label_rows], axis=1)
    arrived = [payload[:capacity]]
    for offset in range(1, seq_count):
        lanes = slice(offset * capacity, (offset + 1) * capacity)
        arrived.append(shift_round(payload[lanes], "seq", offset))
    landed = jnp.concatenate(arrived, axis=0)
    incoming = landed[:, :share_width]
    tags = landed[:, share_width, 0].astype(jnp.int32)
    placement = (tags[None, :] == (page_order + 1)[:, None]).astype(jnp.bfloat16)
    kv_cache = jnp.einsum(
        "ps,sfk->pfk", placement, incoming, preferred_element_type=jnp.float32
    ).astype(jnp.bfloat16)
    return (layer_out, kv_cache)


def solution(mesh):
    placed = (
        P("seq", None),
        P(),
        P("seq", "mp"),
        P(None, "seq", None),
        P("seq", "mp"),
        P("seq"),
        P("seq"),
    )
    return jax.shard_map(
        body,
        mesh=mesh,
        in_specs=placed,
        out_specs=(P("seq", "mp"), P("seq", "mp", None)),
        check_vma=False,
    )
```
